32 devices in a mesh: dp: 2 (over y), pipe: 4 (over z), tensor: 4 (over x, core).
Axes of the slice: x: 2, y: 2, z: 4, core: 2. Of those that a mesh axis runs over, the one named last changes fastest.
Arguments:
- kept_qkv: bfloat16 [2, 4, 3, 192, 6144], P('dp', 'pipe', None, None, 'tensor'), may hold values from -20 to 20
- held_qkv: bfloat16 [2, 4, 3, 192, 6144], P('dp', 'pipe', None, None, 'tensor'), may hold values from -20 to 20
- sent_grad: bfloat16 [2, 4, 2, 64, 6144], P('dp', 'pipe', None, 'tensor'), may hold values from -60 to 60
- order: int32 [2, 4], P('dp', 'pipe'), may hold values from 0 to 1
- offsets: int32 [2, 4, 2], P('dp'), may hold values from 0 to 128, as said below
Outputs:
- query_grad: bfloat16 [2, 4, 2, 64, 6144], P('dp', 'pipe', None, None, 'tensor')
- key_value_grad: bfloat16 [2, 4, 2, 2, 192, 6144], P('dp', 'pipe', None, None, None, 'tensor')
- bias_grad: float32 [4, 3, 6144], P('pipe', None, 'tensor')
The draws below stay inside these ranges and needn't reach their ends.
Inputs may be any that keep to these rules, and one draw needn't show every extreme that they name: `offsets`: multiples of 64.
All inputs are finite; a program needn't handle non-finite values.
Results may differ from the reference program's by a relative error of at most 0.019.
Values may be sent and summed in bfloat16 or wider, within the bound.
No kernel may reach another device: no remote copies, remote signals or barrier semaphores. Data moves between devices by JAX's collectives and lax.ppermute only.
A program may use at most 64 MiB of HBM per device.

```python
import math
import jax
import jax.numpy as jnp
from jax import lax

HEADS = 48
HD = 128
QS = 64
SEQ = 192
FEAT = 6144
N_DP = 2
N_PIPE = 4


def draw_stash(key):
    shape_all = (N_DP, N_PIPE, 3, SEQ, HEADS * HD)
    values_drawn = jax.random.normal(key, shape_all, jnp.float32)
    return jnp.clip(values_drawn, -6.0, 6.0)


def draw_kept_qkv(key, part):
    return draw_stash(jax.random.fold_in(key, 1)).astype(jnp.bfloat16)


def draw_held_qkv(key, part):
    return draw_stash(jax.random.fold_in(key, 2)).astype(jnp.bfloat16)


def draw_offsets(key, part):
    blocks = SEQ // QS
    section_ids = jnp.arange(N_PIPE, dtype=jnp.int32)[None, :, None]
    baseline = ((section_ids + 1) * blocks - 1) // N_PIPE
    extra = jax.random.randint(jax.random.fold_in(key, 3), (N_DP, N_PIPE, 2), 0, 2)
    return (jnp.minimum(baseline + extra, blocks - 1) * QS).astype(jnp.int32)


def plant(drawn, key, least, top_value):
    longest = drawn.shape.index(max(drawn.shape))
    spots = []
    for shift in (0, 1):
        where = [jax.random.randint(jax.random.fold_in(key, axis), (), 0, length) for axis, length in enumerate(drawn.shape)]
        where[longest] = (where[longest] + shift) % drawn.shape[longest]
        spots.append(tuple(where))
    return drawn.at[spots[0]].set(least).at[spots[1]].set(top_value)


def steps_of(key, shape, cuts, smallest, largest):
    loudness, own = 1.0, jax.random.fold_in(key, 6)
    for dim, shards_of in cuts:
        steps = jnp.exp(jax.random.uniform(jax.random.fold_in(own, dim), (shards_of,), jnp.float32, smallest / len(cuts), largest / len(cuts)))
        loudness = loudness * jnp.repeat(steps, shape[dim] // shards_of).reshape([-1 if axis == dim else 1 for axis in range(len(shape))])
    return loudness


def gaussian(own_key, shape, deviation, most, pieces=(), held_as=jnp.bfloat16):
    values = jax.random.normal(own_key, shape, jnp.float32) * deviation
    if len(pieces) > 0:
        values = steps_of(own_key, shape, pieces, -0.22, 0.18) * values
    return jnp.clip(values, min=-most, max=most).astype(held_as)


def setup_inputs(seed: int = 0) -> dict:
    seeds = jax.random.split(jax.random.key(seed), 6)
    return {
        "kept_qkv": draw_kept_qkv(jax.random.fold_in(seeds[5], 71), 0),
        "held_qkv": draw_held_qkv(jax.random.fold_in(seeds[5], 71), 0),
        "sent_grad": gaussian(seeds[2], (N_DP, N_PIPE, 2, QS, FEAT), 10.0, 60.0, ((0, 2), (1, 4), (3, 4))),
        "order": plant(jax.random.randint(seeds[3], (N_DP, N_PIPE), 0, 2), jax.random.fold_in(seeds[3], 1), 0, 1).astype(jnp.int32),
        "offsets": draw_offsets(jax.random.fold_in(seeds[5], 71), 0),
    }


MASK_FILL = -1e+30

def to_bfloat(values_in):
    return lax.optimization_barrier(values_in.astype(jnp.bfloat16)).astype(jnp.float32)

def slice_backward(stash, grad_out, offset):
    key_count = stash.shape[1]
    row_count = grad_out.shape[0]
    feature_count = stash.shape[2]
    head_count = feature_count // HD
    score_scale = 1.0 / math.sqrt(HD)
    queries = lax.dynamic_slice_in_dim(stash[0], offset, row_count, 0).reshape(row_count, head_count, HD).astype(jnp.float32)
    key_rows = stash[1].reshape(key_count, head_count, HD).astype(jnp.float32)
    value_rows = stash[2].reshape(key_count, head_count, HD).astype(jnp.float32)
    out_grad = grad_out.reshape(row_count, head_count, HD).astype(jnp.float32)
    positions = offset + jnp.arange(row_count, dtype=jnp.int32)
    columns = jnp.arange(key_count, dtype=jnp.int32)
    visible = columns[None, :] <= positions[:, None]
    scores = jnp.einsum('qhd,khd->hqk', queries, key_rows) * score_scale
    scores = jnp.where(visible[None], scores, MASK_FILL)
    row_max = lax.optimization_barrier(jnp.max(scores, axis=-1, keepdims=True))
    expos = jnp.exp(scores - row_max)
    attention = expos / lax.optimization_barrier(jnp.sum(expos, axis=-1, keepdims=True))
    attention_low = to_bfloat(attention)
    context = to_bfloat(jnp.einsum('hqk,khd->qhd', attention_low, value_rows))
    delta = lax.optimization_barrier(jnp.sum(out_grad * context, axis=-1)).T
    value_grad = jnp.einsum('hqk,qhd->khd', attention_low, out_grad).astype(jnp.bfloat16)
    prob_grad = jnp.einsum('qhd,khd->hqk', out_grad, value_rows)
    score_grad = to_bfloat(attention * (prob_grad - delta[:, :, None]) * score_scale)
    query_grad = jnp.einsum('hqk,khd->qhd', score_grad, key_rows).astype(jnp.bfloat16)
    key_grad = jnp.einsum('hqk,qhd->khd', score_grad, queries).astype(jnp.bfloat16)
    both_grads = jnp.stack([key_grad.reshape(key_count, feature_count), value_grad.reshape(key_count, feature_count)])
    return (query_grad.reshape(row_count, feature_count), both_grads)

def run_one(item):
    return slice_backward(item[0], item[1], item[2])

def reference(kept_qkv, held_qkv, sent_grad, order, offsets):
    incoming = jnp.roll(sent_grad, -1, axis=1)
    kept_first = (order == 0)[:, :, None, None]
    grad_kept = jnp.where(kept_first, incoming[:, :, 0], incoming[:, :, 1])
    grad_held = jnp.where(kept_first, incoming[:, :, 1], incoming[:, :, 0])
    owned_held = jnp.roll(held_qkv, -(N_PIPE // 2), axis=1)
    flat_count = N_DP * N_PIPE
    kept_q, kept_kv = lax.map(run_one, (kept_qkv.reshape(flat_count, 3, SEQ, FEAT), grad_kept.reshape(flat_count, QS, FEAT), offsets[:, :, 0].reshape(flat_count)))
    held_q, held_kv = lax.map(run_one, (owned_held.reshape(flat_count, 3, SEQ, FEAT), grad_held.reshape(flat_count, QS, FEAT), offsets[:, :, 1].reshape(flat_count)))
    query_grad = jnp.stack([kept_q, held_q], axis=1).reshape(N_DP, N_PIPE, 2, QS, FEAT)
    key_value_grad = jnp.stack([kept_kv, held_kv], axis=1).reshape(N_DP, N_PIPE, 2, 2, SEQ, FEAT)
    query_sums = lax.optimization_barrier(jnp.sum(query_grad.astype(jnp.float32), axis=(0, 2, 3)))
    key_sums = lax.optimization_barrier(jnp.sum(key_value_grad[:, :, :, 0].astype(jnp.float32), axis=(0, 2, 3)))
    value_sums = lax.optimization_barrier(jnp.sum(key_value_grad[:, :, :, 1].astype(jnp.float32), axis=(0, 2, 3)))
    bias_grad = jnp.stack([query_sums, key_sums, value_sums], axis=1)
    return (query_grad, key_value_grad, bias_grad)
```

```python
import math

import jax
import jax.numpy as jnp
from jax import lax
from jax.experimental import pallas as pl
from jax.experimental.pallas import tpu as pltpu
from jax.sharding import PartitionSpec as P

HD = 128
MASK_FILL = -1e30
MAX_CHUNKS = 4
NT_DIMS = (((1,), (1,)), ((), ()))


def from_behind(value, axis, steps):
    count = lax.axis_size(axis)
    pairs = [(source, (source + steps) % count) for source in range(count)]
    return lax.ppermute(value, axis, pairs)


def head_backward(q, k, v, g, visible):
    f32, bf16 = jnp.float32, jnp.bfloat16
    scale = 1.0 / math.sqrt(HD)
    s = lax.dot_general(q, k, NT_DIMS, preferred_element_type=f32) * scale
    s = jnp.where(visible, s, MASK_FILL)
    m = jnp.max(s, axis=1, keepdims=True)
    e = jnp.exp(s - m)
    p = e / jnp.sum(e, axis=1, keepdims=True)
    p_low = p.astype(bf16)
    ctx = jnp.dot(p_low, v, preferred_element_type=f32).astype(bf16)
    delta = jnp.sum(g.astype(f32) * ctx.astype(f32), axis=1, keepdims=True)
    dp = lax.dot_general(g, v, NT_DIMS, preferred_element_type=f32)
    ds = (p * (dp - delta) * scale).astype(bf16)
    dq = jnp.dot(ds, k, preferred_element_type=f32).astype(bf16)
    dk = jnp.dot(ds.T, q, preferred_element_type=f32).astype(bf16)
    dv = jnp.dot(p_low.T, g, preferred_element_type=f32).astype(bf16)
    return dq, dk, dv


def backward_kernel(sliced, off_ref, x_ref, g_ref, dq_ref, dk_ref, dv_ref, sum_ref):
    offset = off_ref[0]
    rows = g_ref.shape[0]
    keys = dk_ref.shape[0]
    heads = g_ref.shape[1] // HD
    pos = offset + lax.broadcasted_iota(jnp.int32, (rows, keys), 0)
    col = lax.broadcasted_iota(jnp.int32, (rows, keys), 1)
    visible = col <= pos
    f32 = jnp.float32

    def head(h, carry):
        cols = pl.ds(pl.multiple_of(h * HD, HD), HD)
        if sliced:
            q = x_ref[pl.ds(0, rows), cols]
            k = x_ref[pl.ds(rows, keys), cols]
            v = x_ref[pl.ds(rows + keys, keys), cols]
        else:
            start = pl.multiple_of(offset, 16)
            q = x_ref[0, pl.ds(start, rows), cols]
            k = x_ref[1, :, cols]
            v = x_ref[2, :, cols]
        g = g_ref[:, cols]
        dq, dk, dv = head_backward(q, k, v, g, visible)
        dq_ref[:, cols] = dq
        dk_ref[:, cols] = dk
        dv_ref[:, cols] = dv
        sum_ref[pl.ds(0, 1), cols] = jnp.sum(dq.astype(f32), axis=0, keepdims=True)
        sum_ref[pl.ds(1, 1), cols] = jnp.sum(dk.astype(f32), axis=0, keepdims=True)
        sum_ref[pl.ds(2, 1), cols] = jnp.sum(dv.astype(f32), axis=0, keepdims=True)
        return carry

    lax.fori_loop(0, heads, head, 0)


def slice_backward(x, g, offset, sliced):
    rows, feats = g.shape
    keys = (x.shape[0] - rows) // 2 if sliced else x.shape[1]
    heads = feats // HD
    bf16 = jnp.bfloat16
    out_shape = (
        jax.ShapeDtypeStruct((rows, feats), bf16),
        jax.ShapeDtypeStruct((keys, feats), bf16),
        jax.ShapeDtypeStruct((keys, feats), bf16),
        jax.ShapeDtypeStruct((3, feats), jnp.float32),
    )
    vmem = pl.BlockSpec(memory_space=pltpu.VMEM)
    cost = pl.CostEstimate(
        flops=heads * 12 * rows * keys * HD,
        transcendentals=heads * rows * keys,
        bytes_accessed=2 * feats * (3 * rows + 4 * keys),
    )
    kernel = lambda *refs: backward_kernel(sliced, *refs)
    return pl.pallas_call(
        kernel,
        out_shape=out_shape,
        in_specs=[pl.BlockSpec(memory_space=pltpu.SMEM), vmem, vmem],
        out_specs=(vmem, vmem, vmem, vmem),
        cost_estimate=cost,
        name="slice_backward",
    )(jnp.reshape(offset, (1,)).astype(jnp.int32), x, g)


def chunk_count(heads):
    for count in range(min(MAX_CHUNKS, heads), 0, -1):
        if heads % count == 0:
            return count
    return 1


def body(kept_qkv, held_qkv, sent_grad, order, offsets):
    section_count = lax.axis_size("pipe")
    half_way = section_count // 2
    section_index = lax.axis_index("pipe")
    feats = kept_qkv.shape[-1]
    keys = kept_qkv.shape[-2]
    heads = feats // HD

    owner = (section_index + section_count - half_way) % section_count
    owner_offset = lax.dynamic_index_in_dim(offsets[0], owner, 0, keepdims=False)[1]
    rows = sent_grad.shape[3] * lax.axis_size("tensor")
    held = held_qkv[0, 0]
    held_q = lax.dynamic_slice_in_dim(held[0], owner_offset, rows, 0)
    packed = jnp.concatenate([held_q, held[1], held[2]], axis=0)
    chunks = chunk_count(heads)
    width = feats // chunks
    parts = packed.reshape(packed.shape[0], chunks, width).transpose(1, 0, 2)
    fetched = [from_behind(parts[c], "pipe", half_way) for c in range(chunks)]

    arrived = from_behind(sent_grad[0, 0], "pipe", -1)
    tensor_count = lax.axis_size("tensor")
    local_rows = arrived.shape[1]
    split = arrived.reshape(2, local_rows, tensor_count, feats).transpose(2, 0, 1, 3)
    regrouped = lax.all_to_all(split, "tensor", split_axis=0, concat_axis=0, tiled=True)
    regrouped = regrouped.transpose(1, 0, 2, 3).reshape(2, rows, feats)
    pick = order[0, 0]
    grad_kept = lax.dynamic_index_in_dim(regrouped, pick, 0, keepdims=False)
    grad_held = lax.dynamic_index_in_dim(regrouped, 1 - pick, 0, keepdims=False)

    section_offsets = lax.dynamic_index_in_dim(offsets[0], section_index, 0, keepdims=False)
    kept_q, kept_k, kept_v, kept_sums = slice_backward(
        kept_qkv[0, 0], grad_kept, section_offsets[0], sliced=False
    )
    held_parts = []
    for c in range(chunks):
        g_part = grad_held[:, c * width:(c + 1) * width]
        held_parts.append(slice_backward(fetched[c], g_part, section_offsets[1], sliced=True))
    held_q = jnp.concatenate([part[0] for part in held_parts], axis=1)
    held_k = jnp.concatenate([part[1] for part in held_parts], axis=1)
    held_v = jnp.concatenate([part[2] for part in held_parts], axis=1)
    held_sums = jnp.concatenate([part[3] for part in held_parts], axis=1)

    query_grad = jnp.stack([kept_q, held_q])
    key_value_grad = jnp.stack([jnp.stack([kept_k, kept_v]), jnp.stack([held_k, held_v])])
    column_sums = kept_sums + held_sums
    if lax.axis_size("dp") == 2:
        bias_grad = column_sums + from_behind(column_sums, "dp", 1)
    else:
        bias_grad = lax.psum(column_sums, "dp")
    return (query_grad[None, None], key_value_grad[None, None], bias_grad[None])


def solution(mesh):
    return jax.shard_map(
        body,
        mesh=mesh,
        in_specs=(
            P("dp", "pipe", None, None, "tensor"),
            P("dp", "pipe", None, None, "tensor"),
            P("dp", "pipe", None, "tensor", None),
            P("dp", "pipe"),
            P("dp", None, None),
        ),
        out_specs=(
            P("dp", "pipe", None, None, "tensor"),
            P("dp", "pipe", None, None, None, "tensor"),
            P("pipe", None, "tensor"),
        ),
        check_vma=False,
    )
```

```python
import math

import jax
import jax.numpy as jnp
from jax import lax
from jax.experimental import pallas as pl
from jax.experimental.pallas import tpu as pltpu
from jax.sharding import PartitionSpec as P

HD = 128
MASK_FILL = -1e30
MAX_CHUNKS = 4
NT_DIMS = (((1,), (1,)), ((), ()))


def from_behind(value, axis, steps):
    count = lax.axis_size(axis)
    pairs = [(source, (source + steps) % count) for source in range(count)]
    return lax.ppermute(value, axis, pairs)


def head_backward(q, k, v, g, visible):
    f32, bf16 = jnp.float32, jnp.bfloat16
    scale = 1.0 / math.sqrt(HD)
    s = lax.dot_general(q, k, NT_DIMS, preferred_element_type=f32) * scale
    s = jnp.where(visible, s, MASK_FILL)
    m = jnp.max(s, axis=1, keepdims=True)
    e = jnp.exp(s - m)
    p = e / jnp.sum(e, axis=1, keepdims=True)
    p_low = p.astype(bf16)
    ctx = jnp.dot(p_low, v, preferred_element_type=f32).astype(bf16)
    delta = jnp.sum(g.astype(f32) * ctx.astype(f32), axis=1, keepdims=True)
    dp = lax.dot_general(g, v, NT_DIMS, preferred_element_type=f32)
    ds = (p * (dp - delta) * scale).astype(bf16)
    dq = jnp.dot(ds, k, preferred_element_type=f32).astype(bf16)
    dk = jnp.dot(ds.T, q, preferred_element_type=f32).astype(bf16)
    dv = jnp.dot(p_low.T, g, preferred_element_type=f32).astype(bf16)
    return dq, dk, dv


def head_loop(offset, load, store):
    rows, keys, heads = load.rows, load.keys, load.heads
    pos = offset + lax.broadcasted_iota(jnp.int32, (rows, keys), 0)
    col = lax.broadcasted_iota(jnp.int32, (rows, keys), 1)
    visible = col <= pos

    def head(h, carry):
        cols = pl.ds(pl.multiple_of(h * HD, HD), HD)
        q, k, v, g = load(cols)
        store(cols, *head_backward(q, k, v, g, visible))
        return carry

    lax.fori_loop(0, heads, head, 0)


class Loader:
    def __init__(self, fn, rows, keys, heads):
        self.fn, self.rows, self.keys, self.heads = fn, rows, keys, heads

    def __call__(self, cols):
        return self.fn(cols)


def store_into(qg_ref, kv_ref, sum_ref, add):
    f32 = jnp.float32

    def store(cols, dq, dk, dv):
        qg_ref[:, cols] = dq
        kv_ref[0, :, cols] = dk
        kv_ref[1, :, cols] = dv
        for row, value in enumerate((dq, dk, dv)):
            total = jnp.sum(value.astype(f32), axis=0, keepdims=True)
            if add:
                total = sum_ref[pl.ds(row, 1), cols] + total
            sum_ref[pl.ds(row, 1), cols] = total

    return store


def kept_kernel(meta_ref, x_ref, g_ref, qg_ref, kv_ref, sum_ref):
    offset = meta_ref[0]
    rows, feats = g_ref.shape
    keys = x_ref.shape[1]
    start = pl.multiple_of(offset, 16)
    load = Loader(
        lambda cols: (x_ref[0, pl.ds(start, rows), cols], x_ref[1, :, cols], x_ref[2, :, cols], g_ref[:, cols]),
        rows, keys, feats // HD,
    )
    head_loop(offset, load, store_into(qg_ref, kv_ref, sum_ref, add=False))


def held_kernel(meta_ref, x_ref, g_ref, qg_in, kv_in, sum_in, qg_ref, kv_ref, sum_ref):
    del qg_in, kv_in
    offset = meta_ref[0]
    rows, feats = g_ref.shape
    keys = (x_ref.shape[0] - rows) // 2
    load = Loader(
        lambda cols: (x_ref[pl.ds(0, rows), cols], x_ref[pl.ds(rows, keys), cols],
                      x_ref[pl.ds(rows + keys, keys), cols], g_ref[:, cols]),
        rows, keys, feats // HD,
    )
    sum_ref[...] = sum_in[...]
    head_loop(offset, load, store_into(qg_ref, kv_ref, sum_ref, add=True))


def kernel_cost(rows, keys, feats):
    heads = feats // HD
    return pl.CostEstimate(
        flops=heads * 12 * rows * keys * HD,
        transcendentals=heads * rows * keys,
        bytes_accessed=2 * feats * (3 * rows + 4 * keys),
    )


def kept_backward(stash, grads, offset, pick):
    _, keys, feats = stash.shape
    rows = grads.shape[1]
    bf16 = jnp.bfloat16
    out_shape = (
        jax.ShapeDtypeStruct((2, rows, feats), bf16),
        jax.ShapeDtypeStruct((2, 2, keys, feats), bf16),
        jax.ShapeDtypeStruct((3, feats), jnp.float32),
    )
    grid_spec = pltpu.PrefetchScalarGridSpec(
        num_scalar_prefetch=1,
        grid=(1,),
        in_specs=[
            pl.BlockSpec((3, keys, feats), lambda i, m: (0, 0, 0)),
            pl.BlockSpec((None, rows, feats), lambda i, m: (m[1], 0, 0)),
        ],
        out_specs=(
            pl.BlockSpec((None, rows, feats), lambda i, m: (0, 0, 0)),
            pl.BlockSpec((None, 2, keys, feats), lambda i, m: (0, 0, 0, 0)),
            pl.BlockSpec((3, feats), lambda i, m: (0, 0)),
        ),
    )
    meta = jnp.stack([offset, pick]).astype(jnp.int32)
    return pl.pallas_call(
        kept_kernel,
        out_shape=out_shape,
        grid_spec=grid_spec,
        cost_estimate=kernel_cost(rows, keys, feats),
        name="kept_backward",
    )(meta, stash, grads)


def held_backward(part, grads, offset, pick, chunk, qg, kv, sums):
    rows = grads.shape[1]
    width = part.shape[1]
    keys = (part.shape[0] - rows) // 2
    grid_spec = pltpu.PrefetchScalarGridSpec(
        num_scalar_prefetch=1,
        grid=(1,),
        in_specs=[
            pl.BlockSpec((part.shape[0], width), lambda i, m: (0, 0)),
            pl.BlockSpec((None, rows, width), lambda i, m: (m[1], 0, chunk)),
            pl.BlockSpec(memory_space=pl.ANY),
            pl.BlockSpec(memory_space=pl.ANY),
            pl.BlockSpec((3, width), lambda i, m: (0, chunk)),
        ],
        out_specs=(
            pl.BlockSpec((None, rows, width), lambda i, m: (1, 0, chunk)),
            pl.BlockSpec((None, 2, keys, width), lambda i, m: (1, 0, 0, chunk)),
            pl.BlockSpec((3, width), lambda i, m: (0, chunk)),
        ),
    )
    meta = jnp.stack([offset, 1 - pick]).astype(jnp.int32)
    return pl.pallas_call(
        held_kernel,
        out_shape=(
            jax.ShapeDtypeStruct(qg.shape, qg.dtype),
            jax.ShapeDtypeStruct(kv.shape, kv.dtype),
            jax.ShapeDtypeStruct(sums.shape, sums.dtype),
        ),
        grid_spec=grid_spec,
        input_output_aliases={3: 0, 4: 1, 5: 2},
        cost_estimate=kernel_cost(rows, keys, width),
        name="held_backward",
    )(meta, part, grads, qg, kv, sums)


def chunk_count(heads):
    for count in range(min(MAX_CHUNKS, heads), 0, -1):
        if heads % count == 0:
            return count
    return 1


def body(kept_qkv, held_qkv, sent_grad, order, offsets):
    section_count = lax.axis_size("pipe")
    half_way = section_count // 2
    section_index = lax.axis_index("pipe")
    feats = kept_qkv.shape[-1]
    keys = kept_qkv.shape[-2]
    heads = feats // HD

    owner = (section_index + section_count - half_way) % section_count
    owner_offset = lax.dynamic_index_in_dim(offsets[0], owner, 0, keepdims=False)[1]
    rows = sent_grad.shape[3] * lax.axis_size("tensor")
    held = held_qkv[0, 0]
    held_q = lax.dynamic_slice_in_dim(held[0], owner_offset, rows, 0)
    chunks = chunk_count(heads)
    width = feats // chunks
    fetched = []
    for c in range(chunks):
        cols = slice(c * width, (c + 1) * width)
        part = jnp.concatenate([held_q[:, cols], held[1, :, cols], held[2, :, cols]], axis=0)
        fetched.append(from_behind(part, "pipe", half_way))

    arrived = from_behind(sent_grad[0, 0], "pipe", -1)
    tensor_count = lax.axis_size("tensor")
    local_rows = arrived.shape[1]
    split = arrived.reshape(2, local_rows, tensor_count, feats).transpose(2, 0, 1, 3)
    regrouped = lax.all_to_all(split, "tensor", split_axis=0, concat_axis=0, tiled=True)
    regrouped = regrouped.transpose(1, 0, 2, 3).reshape(2, rows, feats)
    pick = order[0, 0]
    section_offsets = lax.dynamic_index_in_dim(offsets[0], section_index, 0, keepdims=False)
    qg, kv, column_sums = kept_backward(kept_qkv[0, 0], regrouped, section_offsets[0], pick)
    for c in range(chunks):
        qg, kv, column_sums = held_backward(
            fetched[c], regrouped, section_offsets[1], pick, c, qg, kv, column_sums
        )
    query_grad = qg
    key_value_grad = kv
    if lax.axis_size("dp") == 2:
        bias_grad = column_sums + from_behind(column_sums, "dp", 1)
    else:
        bias_grad = lax.psum(column_sums, "dp")
    return (query_grad[None, None], key_value_grad[None, None], bias_grad[None])


def solution(mesh):
    return jax.shard_map(
        body,
        mesh=mesh,
        in_specs=(
            P("dp", "pipe", None, None, "tensor"),
            P("dp", "pipe", None, None, "tensor"),
            P("dp", "pipe", None, "tensor", None),
            P("dp", "pipe"),
            P("dp", None, None),
        ),
        out_specs=(
            P("dp", "pipe", None, None, "tensor"),
            P("dp", "pipe", None, None, None, "tensor"),
            P("pipe", None, "tensor"),
        ),
        check_vma=False,
    )
```

```python
import math

import jax
import jax.numpy as jnp
from jax import lax
from jax.experimental import pallas as pl
from jax.experimental.pallas import tpu as pltpu
from jax.sharding import PartitionSpec as P

HD = 128
MASK_FILL = -1e30
NT_DIMS = (((1,), (1,)), ((), ()))


def from_behind(value, axis, steps):
    count = lax.axis_size(axis)
    pairs = [(source, (source + steps) % count) for source in range(count)]
    return lax.ppermute(value, axis, pairs)


def head_backward(q, k, v, g, visible):
    f32, bf16 = jnp.float32, jnp.bfloat16
    scale = 1.0 / math.sqrt(HD)
    s = lax.dot_general(q, k, NT_DIMS, preferred_element_type=f32) * scale
    s = jnp.where(visible, s, MASK_FILL)
    m = jnp.max(s, axis=1, keepdims=True)
    e = jnp.exp(s - m)
    p = e / jnp.sum(e, axis=1, keepdims=True)
    p_low = p.astype(bf16)
    ctx = jnp.dot(p_low, v, preferred_element_type=f32).astype(bf16)
    delta = jnp.sum(g.astype(f32) * ctx.astype(f32), axis=1, keepdims=True)
    dp = lax.dot_general(g, v, NT_DIMS, preferred_element_type=f32)
    ds = (p * (dp - delta) * scale).astype(bf16)
    dq = jnp.dot(ds, k, preferred_element_type=f32).astype(bf16)
    dk = jnp.dot(ds.T, q, preferred_element_type=f32).astype(bf16)
    dv = jnp.dot(p_low.T, g, preferred_element_type=f32).astype(bf16)
    return dq, dk, dv


def head_loop(offset, load, store):
    rows, keys, heads = load.rows, load.keys, load.heads
    pos = offset + lax.broadcasted_iota(jnp.int32, (rows, keys), 0)
    col = lax.broadcasted_iota(jnp.int32, (rows, keys), 1)
    visible = col <= pos

    def head(h, carry):
        cols = pl.ds(pl.multiple_of(h * HD, HD), HD)
        q, k, v, g = load(cols)
        store(cols, *head_backward(q, k, v, g, visible))
        return carry

    lax.fori_loop(0, heads, head, 0, unroll=True)


class Loader:
    def __init__(self, fn, rows, keys, heads):
        self.fn, self.rows, self.keys, self.heads = fn, rows, keys, heads

    def __call__(self, cols):
        return self.fn(cols)


def store_into(qg_ref, kv_ref, sum_ref, add):
    f32 = jnp.float32

    def store(cols, dq, dk, dv):
        qg_ref[:, cols] = dq
        kv_ref[0, :, cols] = dk
        kv_ref[1, :, cols] = dv
        for row, value in enumerate((dq, dk, dv)):
            total = jnp.sum(value.astype(f32), axis=0, keepdims=True)
            if add:
                total = sum_ref[pl.ds(row, 1), cols] + total
            sum_ref[pl.ds(row, 1), cols] = total

    return store


def kept_kernel(meta_ref, x_ref, g_ref, qg_ref, kv_ref, sum_ref):
    offset = meta_ref[0]
    rows, feats = g_ref.shape
    keys = x_ref.shape[1]
    start = pl.multiple_of(offset, 16)
    load = Loader(
        lambda cols: (x_ref[0, pl.ds(start, rows), cols], x_ref[1, :, cols], x_ref[2, :, cols], g_ref[:, cols]),
        rows, keys, feats // HD,
    )
    head_loop(offset, load, store_into(qg_ref, kv_ref, sum_ref, add=False))


def held_kernel(meta_ref, x_ref, g_ref, qg_in, kv_in, sum_in, qg_ref, kv_ref, sum_ref):
    del qg_in, kv_in
    offset = meta_ref[0]
    rows, feats = g_ref.shape
    keys = (x_ref.shape[0] - rows) // 2
    load = Loader(
        lambda cols: (x_ref[pl.ds(0, rows), cols], x_ref[pl.ds(rows, keys), cols],
                      x_ref[pl.ds(rows + keys, keys), cols], g_ref[:, cols]),
        rows, keys, feats // HD,
    )
    sum_ref[...] = sum_in[...]
    head_loop(offset, load, store_into(qg_ref, kv_ref, sum_ref, add=True))


def kernel_cost(rows, keys, feats):
    heads = feats // HD
    return pl.CostEstimate(
        flops=heads * 12 * rows * keys * HD,
        transcendentals=heads * rows * keys,
        bytes_accessed=2 * feats * (3 * rows + 4 * keys),
    )


def kept_backward(stash, grads, offset, pick):
    _, keys, feats = stash.shape
    rows = grads.shape[1]
    bf16 = jnp.bfloat16
    out_shape = (
        jax.ShapeDtypeStruct((2, rows, feats), bf16),
        jax.ShapeDtypeStruct((2, 2, keys, feats), bf16),
        jax.ShapeDtypeStruct((3, feats), jnp.float32),
    )
    grid_spec = pltpu.PrefetchScalarGridSpec(
        num_scalar_prefetch=1,
        grid=(1,),
        in_specs=[
            pl.BlockSpec((3, keys, feats), lambda i, m: (0, 0, 0)),
            pl.BlockSpec((None, rows, feats), lambda i, m: (m[1], 0, 0)),
        ],
        out_specs=(
            pl.BlockSpec((None, rows, feats), lambda i, m: (0, 0, 0)),
            pl.BlockSpec((None, 2, keys, feats), lambda i, m: (0, 0, 0, 0)),
            pl.BlockSpec((3, feats), lambda i, m: (0, 0)),
        ),
    )
    meta = jnp.stack([offset, pick]).astype(jnp.int32)
    return pl.pallas_call(
        kept_kernel,
        out_shape=out_shape,
        grid_spec=grid_spec,
        cost_estimate=kernel_cost(rows, keys, feats),
        name="kept_backward",
    )(meta, stash, grads)


def held_backward(part, grads, offset, pick, lo, qg, kv, sums):
    rows = grads.shape[1]
    width = part.shape[1]
    keys = (part.shape[0] - rows) // 2
    assert lo % width == 0
    chunk = lo // width
    grid_spec = pltpu.PrefetchScalarGridSpec(
        num_scalar_prefetch=1,
        grid=(1,),
        in_specs=[
            pl.BlockSpec((part.shape[0], width), lambda i, m: (0, 0)),
            pl.BlockSpec((None, rows, width), lambda i, m: (m[1], 0, chunk)),
            pl.BlockSpec(memory_space=pl.ANY),
            pl.BlockSpec(memory_space=pl.ANY),
            pl.BlockSpec((3, width), lambda i, m: (0, chunk)),
        ],
        out_specs=(
            pl.BlockSpec((None, rows, width), lambda i, m: (1, 0, chunk)),
            pl.BlockSpec((None, 2, keys, width), lambda i, m: (1, 0, 0, chunk)),
            pl.BlockSpec((3, width), lambda i, m: (0, chunk)),
        ),
    )
    meta = jnp.stack([offset, 1 - pick]).astype(jnp.int32)
    return pl.pallas_call(
        held_kernel,
        out_shape=(
            jax.ShapeDtypeStruct(qg.shape, qg.dtype),
            jax.ShapeDtypeStruct(kv.shape, kv.dtype),
            jax.ShapeDtypeStruct(sums.shape, sums.dtype),
        ),
        grid_spec=grid_spec,
        input_output_aliases={3: 0, 4: 1, 5: 2},
        cost_estimate=kernel_cost(rows, keys, width),
        name="held_backward",
    )(meta, part, grads, qg, kv, sums)


def body(kept_qkv, held_qkv, sent_grad, order, offsets):
    section_count = lax.axis_size("pipe")
    half_way = section_count // 2
    section_index = lax.axis_index("pipe")
    feats = kept_qkv.shape[-1]
    keys = kept_qkv.shape[-2]
    heads = feats // HD

    owner = (section_index + section_count - half_way) % section_count
    owner_offset = lax.dynamic_index_in_dim(offsets[0], owner, 0, keepdims=False)[1]
    rows = sent_grad.shape[3] * lax.axis_size("tensor")
    held = held_qkv[0, 0]
    held_q = lax.dynamic_slice_in_dim(held[0], owner_offset, rows, 0)
    first = heads - heads // 3
    bounds = [(0, first * HD), (first * HD, feats)]
    fetched = []
    for lo, hi in bounds:
        part = jnp.concatenate([held_q[:, lo:hi], held[1, :, lo:hi], held[2, :, lo:hi]], axis=0)
        if fetched:
            fetched[-1], part = lax.optimization_barrier((fetched[-1], part))
        fetched.append(from_behind(part, "pipe", half_way))

    arrived = from_behind(sent_grad[0, 0], "pipe", -1)
    tensor_count = lax.axis_size("tensor")
    local_rows = arrived.shape[1]
    split = arrived.reshape(2, local_rows, tensor_count, feats).transpose(2, 0, 1, 3)
    regrouped = lax.all_to_all(split, "tensor", split_axis=0, concat_axis=0, tiled=True)
    regrouped = regrouped.transpose(1, 0, 2, 3).reshape(2, rows, feats)
    pick = order[0, 0]
    section_offsets = lax.dynamic_index_in_dim(offsets[0], section_index, 0, keepdims=False)
    qg, kv, column_sums = kept_backward(kept_qkv[0, 0], regrouped, section_offsets[0], pick)
    for (lo, hi), part in zip(bounds, fetched):
        qg, kv, column_sums = held_backward(
            part, regrouped, section_offsets[1], pick, lo, qg, kv, column_sums
        )
    query_grad = qg
    key_value_grad = kv
    if lax.axis_size("dp") == 2:
        bias_grad = column_sums + from_behind(column_sums, "dp", 1)
    else:
        bias_grad = lax.psum(column_sums, "dp")
    return (query_grad[None, None], key_value_grad[None, None], bias_grad[None])


def solution(mesh):
    return jax.shard_map(
        body,
        mesh=mesh,
        in_specs=(
            P("dp", "pipe", None, None, "tensor"),
            P("dp", "pipe", None, None, "tensor"),
            P("dp", "pipe", None, "tensor", None),
            P("dp", "pipe"),
            P("dp", None, None),
        ),
        out_specs=(
            P("dp", "pipe", None, None, "tensor"),
            P("dp", "pipe", None, None, None, "tensor"),
            P("pipe", None, "tensor"),
        ),
        check_vma=False,
    )
```

```python
import math

import jax
import jax.numpy as jnp
from jax import lax
from jax.experimental import pallas as pl
from jax.experimental.pallas import tpu as pltpu
from jax.sharding import PartitionSpec as P

HD = 128
MASK_FILL = -1e30
NT_DIMS = (((1,), (1,)), ((), ()))


def from_behind(value, axis, steps):
    count = lax.axis_size(axis)
    pairs = [(source, (source + steps) % count) for source in range(count)]
    return lax.ppermute(value, axis, pairs)


def head_backward(q, k, v, g, visible):
    f32, bf16 = jnp.float32, jnp.bfloat16
    scale = 1.0 / math.sqrt(HD)
    s = lax.dot_general(q, k, NT_DIMS, preferred_element_type=f32) * scale
    s = jnp.where(visible, s, MASK_FILL)
    m = jnp.max(s, axis=1, keepdims=True)
    e = jnp.exp(s - m)
    p = e / jnp.sum(e, axis=1, keepdims=True)
    p_low = p.astype(bf16)
    ctx = jnp.dot(p_low, v, preferred_element_type=f32).astype(bf16)
    delta = jnp.sum(g.astype(f32) * ctx.astype(f32), axis=1, keepdims=True)
    dp = lax.dot_general(g, v, NT_DIMS, preferred_element_type=f32)
    ds = (p * (dp - delta) * scale).astype(bf16)
    dq = jnp.dot(ds, k, preferred_element_type=f32).astype(bf16)
    dk = jnp.dot(ds.T, q, preferred_element_type=f32).astype(bf16)
    dv = jnp.dot(p_low.T, g, preferred_element_type=f32).astype(bf16)
    return dq, dk, dv


def head_loop(offset, load, store):
    rows, keys, heads = load.rows, load.keys, load.heads
    pos = offset + lax.broadcasted_iota(jnp.int32, (rows, keys), 0)
    col = lax.broadcasted_iota(jnp.int32, (rows, keys), 1)
    visible = col <= pos

    def head(h, carry):
        cols = pl.ds(pl.multiple_of(h * HD, HD), HD)
        q, k, v, g = load(cols)
        store(cols, *head_backward(q, k, v, g, visible))
        return carry

    lax.fori_loop(0, heads, head, 0, unroll=True)


class Loader:
    def __init__(self, fn, rows, keys, heads):
        self.fn, self.rows, self.keys, self.heads = fn, rows, keys, heads

    def __call__(self, cols):
        return self.fn(cols)


def store_into(qg_ref, kv_ref, sum_ref, add):
    f32 = jnp.float32

    def store(cols, dq, dk, dv):
        qg_ref[:, cols] = dq
        kv_ref[0, :, cols] = dk
        kv_ref[1, :, cols] = dv
        for row, value in enumerate((dq, dk, dv)):
            total = jnp.sum(value.astype(f32), axis=0, keepdims=True)
            if add:
                total = sum_ref[pl.ds(row, 1), cols] + total
            sum_ref[pl.ds(row, 1), cols] = total

    return store


def kept_kernel(meta_ref, x_ref, g_ref, qg_ref, kv_ref, sum_ref):
    offset = meta_ref[0]
    rows, feats = g_ref.shape
    keys = x_ref.shape[1]
    start = pl.multiple_of(offset, 16)
    load = Loader(
        lambda cols: (x_ref[0, pl.ds(start, rows), cols], x_ref[1, :, cols], x_ref[2, :, cols], g_ref[:, cols]),
        rows, keys, feats // HD,
    )
    head_loop(offset, load, store_into(qg_ref, kv_ref, sum_ref, add=False))


def held_kernel(meta_ref, x_ref, g_ref, qg_in, kv_in, sum_in, qg_ref, kv_ref, sum_ref):
    del qg_in, kv_in
    offset = meta_ref[0]
    rows, feats = g_ref.shape
    keys = (x_ref.shape[0] - rows) // 2
    load = Loader(
        lambda cols: (x_ref[pl.ds(0, rows), cols], x_ref[pl.ds(rows, keys), cols],
                      x_ref[pl.ds(rows + keys, keys), cols], g_ref[:, cols]),
        rows, keys, feats // HD,
    )
    sum_ref[...] = sum_in[...]
    head_loop(offset, load, store_into(qg_ref, kv_ref, sum_ref, add=True))


def kernel_cost(rows, keys, feats):
    heads = feats // HD
    return pl.CostEstimate(
        flops=heads * 12 * rows * keys * HD,
        transcendentals=heads * rows * keys,
        bytes_accessed=2 * feats * (3 * rows + 4 * keys),
    )


def kept_backward(stash, grads, offset, pick):
    _, keys, feats = stash.shape
    rows = grads.shape[1]
    bf16 = jnp.bfloat16
    out_shape = (
        jax.ShapeDtypeStruct((2, rows, feats), bf16),
        jax.ShapeDtypeStruct((2, 2, keys, feats), bf16),
        jax.ShapeDtypeStruct((3, feats), jnp.float32),
    )
    grid_spec = pltpu.PrefetchScalarGridSpec(
        num_scalar_prefetch=1,
        grid=(1,),
        in_specs=[
            pl.BlockSpec((3, keys, feats), lambda i, m: (0, 0, 0)),
            pl.BlockSpec((None, rows, feats), lambda i, m: (m[1], 0, 0)),
        ],
        out_specs=(
            pl.BlockSpec((None, rows, feats), lambda i, m: (0, 0, 0)),
            pl.BlockSpec((None, 2, keys, feats), lambda i, m: (0, 0, 0, 0)),
            pl.BlockSpec((3, feats), lambda i, m: (0, 0)),
        ),
    )
    meta = jnp.stack([offset, pick]).astype(jnp.int32)
    return pl.pallas_call(
        kept_kernel,
        out_shape=out_shape,
        grid_spec=grid_spec,
        cost_estimate=kernel_cost(rows, keys, feats),
        name="kept_backward",
    )(meta, stash, grads)


def held_backward(part, grads, offset, pick, lo, qg, kv, sums):
    rows = grads.shape[1]
    width = part.shape[1]
    keys = (part.shape[0] - rows) // 2
    assert lo % width == 0
    chunk = lo // width
    grid_spec = pltpu.PrefetchScalarGridSpec(
        num_scalar_prefetch=1,
        grid=(1,),
        in_specs=[
            pl.BlockSpec((part.shape[0], width), lambda i, m: (0, 0)),
            pl.BlockSpec((None, rows, width), lambda i, m: (m[1], 0, chunk)),
            pl.BlockSpec(memory_space=pl.ANY),
            pl.BlockSpec(memory_space=pl.ANY),
            pl.BlockSpec((3, width), lambda i, m: (0, chunk)),
        ],
        out_specs=(
            pl.BlockSpec((None, rows, width), lambda i, m: (1, 0, chunk)),
            pl.BlockSpec((None, 2, keys, width), lambda i, m: (1, 0, 0, chunk)),
            pl.BlockSpec((3, width), lambda i, m: (0, chunk)),
        ),
    )
    meta = jnp.stack([offset, 1 - pick]).astype(jnp.int32)
    return pl.pallas_call(
        held_kernel,
        out_shape=(
            jax.ShapeDtypeStruct(qg.shape, qg.dtype),
            jax.ShapeDtypeStruct(kv.shape, kv.dtype),
            jax.ShapeDtypeStruct(sums.shape, sums.dtype),
        ),
        grid_spec=grid_spec,
        input_output_aliases={3: 0, 4: 1, 5: 2},
        cost_estimate=kernel_cost(rows, keys, width),
        name="held_backward",
    )(meta, part, grads, qg, kv, sums)


def body(kept_qkv, held_qkv, sent_grad, order, offsets):
    section_count = lax.axis_size("pipe")
    half_way = section_count // 2
    section_index = lax.axis_index("pipe")
    feats = kept_qkv.shape[-1]
    keys = kept_qkv.shape[-2]
    heads = feats // HD

    owner = (section_index + section_count - half_way) % section_count
    owner_offset = lax.dynamic_index_in_dim(offsets[0], owner, 0, keepdims=False)[1]
    rows = sent_grad.shape[3] * lax.axis_size("tensor")
    held = held_qkv[0, 0]
    held_q = lax.dynamic_slice_in_dim(held[0], owner_offset, rows, 0)
    first = heads - max(1, heads // 6)
    bounds = [(0, first * HD), (first * HD, feats)]
    parts = [
        jnp.concatenate([held_q[:, lo:hi], held[1, :, lo:hi], held[2, :, lo:hi]], axis=0)
        for lo, hi in bounds
    ]
    fetched_first = from_behind(parts[0], "pipe", half_way)

    arrived = from_behind(sent_grad[0, 0], "pipe", -1)
    tensor_count = lax.axis_size("tensor")
    local_rows = arrived.shape[1]
    split = arrived.reshape(2, local_rows, tensor_count, feats).transpose(2, 0, 1, 3)
    regrouped = lax.all_to_all(split, "tensor", split_axis=0, concat_axis=0, tiled=True)
    regrouped = regrouped.transpose(1, 0, 2, 3).reshape(2, rows, feats)
    pick = order[0, 0]
    section_offsets = lax.dynamic_index_in_dim(offsets[0], section_index, 0, keepdims=False)
    qg, kv, column_sums = kept_backward(kept_qkv[0, 0], regrouped, section_offsets[0], pick)
    fetched_first, second, qg, kv, column_sums = lax.optimization_barrier(
        (fetched_first, parts[1], qg, kv, column_sums)
    )
    fetched = [fetched_first, from_behind(second, "pipe", half_way)]
    for (lo, hi), part in zip(bounds, fetched):
        qg, kv, column_sums = held_backward(
            part, regrouped, section_offsets[1], pick, lo, qg, kv, column_sums
        )
    query_grad = qg
    key_value_grad = kv
    if lax.axis_size("dp") == 2:
        bias_grad = column_sums + from_behind(column_sums, "dp", 1)
    else:
        bias_grad = lax.psum(column_sums, "dp")
    return (query_grad[None, None], key_value_grad[None, None], bias_grad[None])


def solution(mesh):
    return jax.shard_map(
        body,
        mesh=mesh,
        in_specs=(
            P("dp", "pipe", None, None, "tensor"),
            P("dp", "pipe", None, None, "tensor"),
            P("dp", "pipe", None, "tensor", None),
            P("dp", "pipe"),
            P("dp", None, None),
        ),
        out_specs=(
            P("dp", "pipe", None, None, "tensor"),
            P("dp", "pipe", None, None, None, "tensor"),
            P("pipe", None, "tensor"),
        ),
        check_vma=False,
    )
```

```python
import math

import jax
import jax.numpy as jnp
from jax import lax
from jax.experimental import pallas as pl
from jax.experimental.pallas import tpu as pltpu
from jax.sharding import PartitionSpec as P

HD = 128
MASK_FILL = -1e30
MAX_CHUNKS = 1
NT_DIMS = (((1,), (1,)), ((), ()))


def from_behind(value, axis, steps):
    count = lax.axis_size(axis)
    pairs = [(source, (source + steps) % count) for source in range(count)]
    return lax.ppermute(value, axis, pairs)


def head_backward(q, k, v, g, visible):
    f32, bf16 = jnp.float32, jnp.bfloat16
    scale = 1.0 / math.sqrt(HD)
    s = lax.dot_general(q, k, NT_DIMS, preferred_element_type=f32) * scale
    s = jnp.where(visible, s, MASK_FILL)
    m = jnp.max(s, axis=1, keepdims=True)
    e = jnp.exp(s - m)
    p = e / jnp.sum(e, axis=1, keepdims=True)
    p_low = p.astype(bf16)
    ctx = jnp.dot(p_low, v, preferred_element_type=f32).astype(bf16)
    delta = jnp.sum(g.astype(f32) * ctx.astype(f32), axis=1, keepdims=True)
    dp = lax.dot_general(g, v, NT_DIMS, preferred_element_type=f32)
    ds = (p * (dp - delta) * scale).astype(bf16)
    dq = jnp.dot(ds, k, preferred_element_type=f32).astype(bf16)
    dk = jnp.dot(ds.T, q, preferred_element_type=f32).astype(bf16)
    dv = jnp.dot(p_low.T, g, preferred_element_type=f32).astype(bf16)
    return dq, dk, dv


def head_loop(offset, load, store):
    rows, keys, heads = load.rows, load.keys, load.heads
    pos = offset + lax.broadcasted_iota(jnp.int32, (rows, keys), 0)
    col = lax.broadcasted_iota(jnp.int32, (rows, keys), 1)
    visible = col <= pos

    def head(h, carry):
        cols = pl.ds(pl.multiple_of(h * HD, HD), HD)
        q, k, v, g = load(cols)
        store(cols, *head_backward(q, k, v, g, visible))
        return carry

    lax.fori_loop(0, heads, head, 0, unroll=True)


class Loader:
    def __init__(self, fn, rows, keys, heads):
        self.fn, self.rows, self.keys, self.heads = fn, rows, keys, heads

    def __call__(self, cols):
        return self.fn(cols)


def store_into(qg_ref, kv_ref, sum_ref, add):
    f32 = jnp.float32

    def store(cols, dq, dk, dv):
        qg_ref[:, cols] = dq
        kv_ref[0, :, cols] = dk
        kv_ref[1, :, cols] = dv
        for row, value in enumerate((dq, dk, dv)):
            total = jnp.sum(value.astype(f32), axis=0, keepdims=True)
            if add:
                total = sum_ref[pl.ds(row, 1), cols] + total
            sum_ref[pl.ds(row, 1), cols] = total

    return store


def kept_kernel(meta_ref, x_ref, g_ref, qg_ref, kv_ref, sum_ref):
    offset = meta_ref[0]
    rows, feats = g_ref.shape
    keys = x_ref.shape[1]
    start = pl.multiple_of(offset, 16)
    load = Loader(
        lambda cols: (x_ref[0, pl.ds(start, rows), cols], x_ref[1, :, cols], x_ref[2, :, cols], g_ref[:, cols]),
        rows, keys, feats // HD,
    )
    head_loop(offset, load, store_into(qg_ref, kv_ref, sum_ref, add=False))


def held_kernel(meta_ref, x_ref, g_ref, qg_in, kv_in, sum_in, qg_ref, kv_ref, sum_ref):
    del qg_in, kv_in
    offset = meta_ref[0]
    rows, feats = g_ref.shape
    keys = (x_ref.shape[0] - rows) // 2
    load = Loader(
        lambda cols: (x_ref[pl.ds(0, rows), cols], x_ref[pl.ds(rows, keys), cols],
                      x_ref[pl.ds(rows + keys, keys), cols], g_ref[:, cols]),
        rows, keys, feats // HD,
    )
    sum_ref[...] = sum_in[...]
    head_loop(offset, load, store_into(qg_ref, kv_ref, sum_ref, add=True))


def kernel_cost(rows, keys, feats):
    heads = feats // HD
    return pl.CostEstimate(
        flops=heads * 12 * rows * keys * HD,
        transcendentals=heads * rows * keys,
        bytes_accessed=2 * feats * (3 * rows + 4 * keys),
    )


def kept_backward(stash, grads, offset, pick):
    _, keys, feats = stash.shape
    rows = grads.shape[1]
    bf16 = jnp.bfloat16
    out_shape = (
        jax.ShapeDtypeStruct((2, rows, feats), bf16),
        jax.ShapeDtypeStruct((2, 2, keys, feats), bf16),
        jax.ShapeDtypeStruct((3, feats), jnp.float32),
    )
    grid_spec = pltpu.PrefetchScalarGridSpec(
        num_scalar_prefetch=1,
        grid=(1,),
        in_specs=[
            pl.BlockSpec((3, keys, feats), lambda i, m: (0, 0, 0)),
            pl.BlockSpec((None, rows, feats), lambda i, m: (m[1], 0, 0)),
        ],
        out_specs=(
            pl.BlockSpec((None, rows, feats), lambda i, m: (0, 0, 0)),
            pl.BlockSpec((None, 2, keys, feats), lambda i, m: (0, 0, 0, 0)),
            pl.BlockSpec((3, feats), lambda i, m: (0, 0)),
        ),
    )
    meta = jnp.stack([offset, pick]).astype(jnp.int32)
    return pl.pallas_call(
        kept_kernel,
        out_shape=out_shape,
        grid_spec=grid_spec,
        cost_estimate=kernel_cost(rows, keys, feats),
        name="kept_backward",
    )(meta, stash, grads)


def held_backward(part, grads, offset, pick, chunk, qg, kv, sums):
    rows = grads.shape[1]
    width = part.shape[1]
    keys = (part.shape[0] - rows) // 2
    grid_spec = pltpu.PrefetchScalarGridSpec(
        num_scalar_prefetch=1,
        grid=(1,),
        in_specs=[
            pl.BlockSpec((part.shape[0], width), lambda i, m: (0, 0)),
            pl.BlockSpec((None, rows, width), lambda i, m: (m[1], 0, chunk)),
            pl.BlockSpec(memory_space=pl.ANY),
            pl.BlockSpec(memory_space=pl.ANY),
            pl.BlockSpec((3, width), lambda i, m: (0, chunk)),
        ],
        out_specs=(
            pl.BlockSpec((None, rows, width), lambda i, m: (1, 0, chunk)),
            pl.BlockSpec((None, 2, keys, width), lambda i, m: (1, 0, 0, chunk)),
            pl.BlockSpec((3, width), lambda i, m: (0, chunk)),
        ),
    )
    meta = jnp.stack([offset, 1 - pick]).astype(jnp.int32)
    return pl.pallas_call(
        held_kernel,
        out_shape=(
            jax.ShapeDtypeStruct(qg.shape, qg.dtype),
            jax.ShapeDtypeStruct(kv.shape, kv.dtype),
            jax.ShapeDtypeStruct(sums.shape, sums.dtype),
        ),
        grid_spec=grid_spec,
        input_output_aliases={3: 0, 4: 1, 5: 2},
        cost_estimate=kernel_cost(rows, keys, width),
        name="held_backward",
    )(meta, part, grads, qg, kv, sums)


def chunk_count(heads):
    for count in range(min(MAX_CHUNKS, heads), 0, -1):
        if heads % count == 0:
            return count
    return 1


def body(kept_qkv, held_qkv, sent_grad, order, offsets):
    section_count = lax.axis_size("pipe")
    half_way = section_count // 2
    section_index = lax.axis_index("pipe")
    feats = kept_qkv.shape[-1]
    keys = kept_qkv.shape[-2]
    heads = feats // HD

    owner = (section_index + section_count - half_way) % section_count
    owner_offset = lax.dynamic_index_in_dim(offsets[0], owner, 0, keepdims=False)[1]
    rows = sent_grad.shape[3] * lax.axis_size("tensor")
    held = held_qkv[0, 0]
    held_q = lax.dynamic_slice_in_dim(held[0], owner_offset, rows, 0)
    chunks = chunk_count(heads)
    width = feats // chunks
    fetched = []
    for c in range(chunks):
        cols = slice(c * width, (c + 1) * width)
        part = jnp.concatenate([held_q[:, cols], held[1, :, cols], held[2, :, cols]], axis=0)
        fetched.append(from_behind(part, "pipe", half_way))

    arrived = from_behind(sent_grad[0, 0], "pipe", -1)
    tensor_count = lax.axis_size("tensor")
    local_rows = arrived.shape[1]
    split = arrived.reshape(2, local_rows, tensor_count, feats).transpose(2, 0, 1, 3)
    regrouped = lax.all_to_all(split, "tensor", split_axis=0, concat_axis=0, tiled=True)
    regrouped = regrouped.transpose(1, 0, 2, 3).reshape(2, rows, feats)
    pick = order[0, 0]
    section_offsets = lax.dynamic_index_in_dim(offsets[0], section_index, 0, keepdims=False)
    qg, kv, column_sums = kept_backward(kept_qkv[0, 0], regrouped, section_offsets[0], pick)
    for c in range(chunks):
        qg, kv, column_sums = held_backward(
            fetched[c], regrouped, section_offsets[1], pick, c, qg, kv, column_sums
        )
    query_grad = qg
    key_value_grad = kv
    if lax.axis_size("dp") == 2:
        bias_grad = column_sums + from_behind(column_sums, "dp", 1)
    else:
        bias_grad = lax.psum(column_sums, "dp")
    return (query_grad[None, None], key_value_grad[None, None], bias_grad[None])


def solution(mesh):
    return jax.shard_map(
        body,
        mesh=mesh,
        in_specs=(
            P("dp", "pipe", None, None, "tensor"),
            P("dp", "pipe", None, None, "tensor"),
            P("dp", "pipe", None, "tensor", None),
            P("dp", "pipe"),
            P("dp", None, None),
        ),
        out_specs=(
            P("dp", "pipe", None, None, "tensor"),
            P("dp", "pipe", None, None, None, "tensor"),
            P("pipe", None, "tensor"),
        ),
        check_vma=False,
    )
```

```python
import math

import jax
import jax.numpy as jnp
from jax import lax
from jax.experimental import pallas as pl
from jax.experimental.pallas import tpu as pltpu
from jax.sharding import PartitionSpec as P

HD = 128
MASK_FILL = -1e30
MAX_CHUNKS = 4
NT_DIMS = (((1,), (1,)), ((), ()))


def from_behind(value, axis, steps):
    count = lax.axis_size(axis)
    pairs = [(source, (source + steps) % count) for source in range(count)]
    return lax.ppermute(value, axis, pairs)


def head_backward(q, k, v, g, visible):
    f32, bf16 = jnp.float32, jnp.bfloat16
    scale = 1.0 / math.sqrt(HD)
    s = lax.dot_general(q, k, NT_DIMS, preferred_element_type=f32) * scale
    s = jnp.where(visible, s, MASK_FILL)
    m = jnp.max(s, axis=1, keepdims=True)
    e = jnp.exp(s - m)
    p = e / jnp.sum(e, axis=1, keepdims=True)
    p_low = p.astype(bf16)
    ctx = jnp.dot(p_low, v, preferred_element_type=f32).astype(bf16)
    delta = jnp.sum(g.astype(f32) * ctx.astype(f32), axis=1, keepdims=True)
    dp = lax.dot_general(g, v, NT_DIMS, preferred_element_type=f32)
    ds = (p * (dp - delta) * scale).astype(bf16)
    dq = jnp.dot(ds, k, preferred_element_type=f32).astype(bf16)
    dk = jnp.dot(ds.T, q, preferred_element_type=f32).astype(bf16)
    dv = jnp.dot(p_low.T, g, preferred_element_type=f32).astype(bf16)
    return dq, dk, dv


def head_loop(offset, load, store):
    rows, keys, heads = load.rows, load.keys, load.heads
    pos = offset + lax.broadcasted_iota(jnp.int32, (rows, keys), 0)
    col = lax.broadcasted_iota(jnp.int32, (rows, keys), 1)
    visible = col <= pos

    def head(h, carry):
        cols = pl.ds(pl.multiple_of(h * HD, HD), HD)
        q, k, v, g = load(cols)
        store(cols, *head_backward(q, k, v, g, visible))
        return carry

    lax.fori_loop(0, heads, head, 0, unroll=True)


class Loader:
    def __init__(self, fn, rows, keys, heads):
        self.fn, self.rows, self.keys, self.heads = fn, rows, keys, heads

    def __call__(self, cols):
        return self.fn(cols)


def store_into(qg_ref, kv_ref, sum_ref, add):
    f32 = jnp.float32

    def store(cols, dq, dk, dv):
        qg_ref[:, cols] = dq
        kv_ref[0, :, cols] = dk
        kv_ref[1, :, cols] = dv
        for row, value in enumerate((dq, dk, dv)):
            total = jnp.sum(value.astype(f32), axis=0, keepdims=True)
            if add:
                total = sum_ref[pl.ds(row, 1), cols] + total
            sum_ref[pl.ds(row, 1), cols] = total

    return store


def kept_kernel(meta_ref, x_ref, g_ref, qg_ref, kv_ref, sum_ref):
    offset = meta_ref[0]
    rows, feats = g_ref.shape
    keys = x_ref.shape[1]
    start = pl.multiple_of(offset, 16)
    load = Loader(
        lambda cols: (x_ref[0, pl.ds(start, rows), cols], x_ref[1, :, cols], x_ref[2, :, cols], g_ref[:, cols]),
        rows, keys, feats // HD,
    )
    head_loop(offset, load, store_into(qg_ref, kv_ref, sum_ref, add=False))


def held_kernel(meta_ref, x_ref, g_ref, qg_ref, kv_ref, sum_ref):
    offset = meta_ref[0]
    rows, feats = g_ref.shape
    keys = (x_ref.shape[0] - rows) // 2
    load = Loader(
        lambda cols: (x_ref[pl.ds(0, rows), cols], x_ref[pl.ds(rows, keys), cols],
                      x_ref[pl.ds(rows + keys, keys), cols], g_ref[:, cols]),
        rows, keys, feats // HD,
    )
    head_loop(offset, load, store_into(qg_ref, kv_ref, sum_ref, add=False))


def kernel_cost(rows, keys, feats):
    heads = feats // HD
    return pl.CostEstimate(
        flops=heads * 12 * rows * keys * HD,
        transcendentals=heads * rows * keys,
        bytes_accessed=2 * feats * (3 * rows + 4 * keys),
    )


def kept_backward(stash, grads, offset, pick):
    _, keys, feats = stash.shape
    rows = grads.shape[1]
    bf16 = jnp.bfloat16
    out_shape = (
        jax.ShapeDtypeStruct((2, rows, feats), bf16),
        jax.ShapeDtypeStruct((2, 2, keys, feats), bf16),
        jax.ShapeDtypeStruct((3, feats), jnp.float32),
    )
    grid_spec = pltpu.PrefetchScalarGridSpec(
        num_scalar_prefetch=1,
        grid=(1,),
        in_specs=[
            pl.BlockSpec((3, keys, feats), lambda i, m: (0, 0, 0)),
            pl.BlockSpec((None, rows, feats), lambda i, m: (m[1], 0, 0)),
        ],
        out_specs=(
            pl.BlockSpec((None, rows, feats), lambda i, m: (0, 0, 0)),
            pl.BlockSpec((None, 2, keys, feats), lambda i, m: (0, 0, 0, 0)),
            pl.BlockSpec((3, feats), lambda i, m: (0, 0)),
        ),
    )
    meta = jnp.stack([offset, pick]).astype(jnp.int32)
    return pl.pallas_call(
        kept_kernel,
        out_shape=out_shape,
        grid_spec=grid_spec,
        cost_estimate=kernel_cost(rows, keys, feats),
        name="kept_backward",
    )(meta, stash, grads)


def held_backward(part, grads, offset, pick, chunk):
    rows = grads.shape[1]
    width = part.shape[1]
    keys = (part.shape[0] - rows) // 2
    bf16 = jnp.bfloat16
    grid_spec = pltpu.PrefetchScalarGridSpec(
        num_scalar_prefetch=1,
        grid=(1,),
        in_specs=[
            pl.BlockSpec((part.shape[0], width), lambda i, m: (0, 0)),
            pl.BlockSpec((None, rows, width), lambda i, m: (m[1], 0, chunk)),
        ],
        out_specs=(
            pl.BlockSpec((rows, width), lambda i, m: (0, 0)),
            pl.BlockSpec((2, keys, width), lambda i, m: (0, 0, 0)),
            pl.BlockSpec((3, width), lambda i, m: (0, 0)),
        ),
    )
    meta = jnp.stack([offset, 1 - pick]).astype(jnp.int32)
    return pl.pallas_call(
        held_kernel,
        out_shape=(
            jax.ShapeDtypeStruct((rows, width), bf16),
            jax.ShapeDtypeStruct((2, keys, width), bf16),
            jax.ShapeDtypeStruct((3, width), jnp.float32),
        ),
        grid_spec=grid_spec,
        cost_estimate=kernel_cost(rows, keys, width),
        name="held_backward",
    )(meta, part, grads)


def chunk_count(heads):
    for count in range(min(MAX_CHUNKS, heads), 0, -1):
        if heads % count == 0:
            return count
    return 1


def body(kept_qkv, held_qkv, sent_grad, order, offsets):
    section_count = lax.axis_size("pipe")
    half_way = section_count // 2
    section_index = lax.axis_index("pipe")
    feats = kept_qkv.shape[-1]
    keys = kept_qkv.shape[-2]
    heads = feats // HD

    owner = (section_index + section_count - half_way) % section_count
    owner_offset = lax.dynamic_index_in_dim(offsets[0], owner, 0, keepdims=False)[1]
    rows = sent_grad.shape[3] * lax.axis_size("tensor")
    held = held_qkv[0, 0]
    held_q = lax.dynamic_slice_in_dim(held[0], owner_offset, rows, 0)
    chunks = chunk_count(heads)
    width = feats // chunks
    fetched = []
    for c in range(chunks):
        cols = slice(c * width, (c + 1) * width)
        part = jnp.concatenate([held_q[:, cols], held[1, :, cols], held[2, :, cols]], axis=0)
        fetched.append(from_behind(part, "pipe", half_way))

    arrived = from_behind(sent_grad[0, 0], "pipe", -1)
    tensor_count = lax.axis_size("tensor")
    local_rows = arrived.shape[1]
    split = arrived.reshape(2, local_rows, tensor_count, feats).transpose(2, 0, 1, 3)
    regrouped = lax.all_to_all(split, "tensor", split_axis=0, concat_axis=0, tiled=True)
    regrouped = regrouped.transpose(1, 0, 2, 3).reshape(2, rows, feats)
    pick = order[0, 0]
    section_offsets = lax.dynamic_index_in_dim(offsets[0], section_index, 0, keepdims=False)
    qg, kv, column_sums = kept_backward(kept_qkv[0, 0], regrouped, section_offsets[0], pick)
    held_parts = [
        held_backward(fetched[c], regrouped, section_offsets[1], pick, c) for c in range(chunks)
    ]
    for c, (part_q, part_kv, _) in enumerate(held_parts):
        qg = lax.dynamic_update_slice(qg, part_q[None], (1, 0, c * width))
        kv = lax.dynamic_update_slice(kv, part_kv[None], (1, 0, 0, c * width))
    column_sums = column_sums + jnp.concatenate([part[2] for part in held_parts], axis=1)
    query_grad = qg
    key_value_grad = kv
    if lax.axis_size("dp") == 2:
        bias_grad = column_sums + from_behind(column_sums, "dp", 1)
    else:
        bias_grad = lax.psum(column_sums, "dp")
    return (query_grad[None, None], key_value_grad[None, None], bias_grad[None])


def solution(mesh):
    return jax.shard_map(
        body,
        mesh=mesh,
        in_specs=(
            P("dp", "pipe", None, None, "tensor"),
            P("dp", "pipe", None, None, "tensor"),
            P("dp", "pipe", None, "tensor", None),
            P("dp", "pipe"),
            P("dp", None, None),
        ),
        out_specs=(
            P("dp", "pipe", None, None, "tensor"),
            P("dp", "pipe", None, None, None, "tensor"),
            P("pipe", None, "tensor"),
        ),
        check_vma=False,
    )
```

```python
import math

import jax
import jax.numpy as jnp
from jax import lax
from jax.experimental import pallas as pl
from jax.experimental.pallas import tpu as pltpu
from jax.sharding import PartitionSpec as P

HD = 128
MASK_FILL = -1e30
MAX_CHUNKS = 4
NT_DIMS = (((1,), (1,)), ((), ()))


def from_behind(value, axis, steps):
    count = lax.axis_size(axis)
    pairs = [(source, (source + steps) % count) for source in range(count)]
    return lax.ppermute(value, axis, pairs)


def head_backward(q, k, v, g, visible):
    f32, bf16 = jnp.float32, jnp.bfloat16
    scale = 1.0 / math.sqrt(HD)
    s = lax.dot_general(q, k, NT_DIMS, preferred_element_type=f32) * scale
    s = jnp.where(visible, s, MASK_FILL)
    m = jnp.max(s, axis=1, keepdims=True)
    e = jnp.exp(s - m)
    p = e / jnp.sum(e, axis=1, keepdims=True)
    p_low = p.astype(bf16)
    ctx = jnp.dot(p_low, v, preferred_element_type=f32).astype(bf16)
    delta = jnp.sum(g.astype(f32) * ctx.astype(f32), axis=1, keepdims=True)
    dp = lax.dot_general(g, v, NT_DIMS, preferred_element_type=f32)
    ds = (p * (dp - delta) * scale).astype(bf16)
    dq = jnp.dot(ds, k, preferred_element_type=f32).astype(bf16)
    dk = jnp.dot(ds.T, q, preferred_element_type=f32).astype(bf16)
    dv = jnp.dot(p_low.T, g, preferred_element_type=f32).astype(bf16)
    return dq, dk, dv


def head_loop(offset, load, store):
    rows, keys, heads = load.rows, load.keys, load.heads
    pos = offset + lax.broadcasted_iota(jnp.int32, (rows, keys), 0)
    col = lax.broadcasted_iota(jnp.int32, (rows, keys), 1)
    visible = col <= pos

    def head(h, carry):
        cols = pl.ds(pl.multiple_of(h * HD, HD), HD)
        q, k, v, g = load(cols)
        store(cols, *head_backward(q, k, v, g, visible))
        return carry

    lax.fori_loop(0, heads, head, 0, unroll=True)


class Loader:
    def __init__(self, fn, rows, keys, heads):
        self.fn, self.rows, self.keys, self.heads = fn, rows, keys, heads

    def __call__(self, cols):
        return self.fn(cols)


def store_into(qg_ref, kv_ref, sum_ref, add):
    f32 = jnp.float32

    def store(cols, dq, dk, dv):
        qg_ref[:, cols] = dq
        kv_ref[0, :, cols] = dk
        kv_ref[1, :, cols] = dv
        for row, value in enumerate((dq, dk, dv)):
            total = jnp.sum(value.astype(f32), axis=0, keepdims=True)
            if add:
                total = sum_ref[pl.ds(row, 1), cols] + total
            sum_ref[pl.ds(row, 1), cols] = total

    return store


def kept_kernel(meta_ref, x_ref, g_ref, qg_ref, kv_ref, sum_ref):
    offset = meta_ref[0]
    rows, feats = g_ref.shape
    keys = x_ref.shape[1]
    start = pl.multiple_of(offset, 16)
    load = Loader(
        lambda cols: (x_ref[0, pl.ds(start, rows), cols], x_ref[1, :, cols], x_ref[2, :, cols], g_ref[:, cols]),
        rows, keys, feats // HD,
    )
    head_loop(offset, load, store_into(qg_ref, kv_ref, sum_ref, add=False))


def held_kernel(meta_ref, x_ref, g_ref, qg_ref, kv_ref, sum_ref):
    offset = meta_ref[0]
    rows, feats = g_ref.shape
    keys = (x_ref.shape[0] - rows) // 2
    load = Loader(
        lambda cols: (x_ref[pl.ds(0, rows), cols], x_ref[pl.ds(rows, keys), cols],
                      x_ref[pl.ds(rows + keys, keys), cols], g_ref[:, cols]),
        rows, keys, feats // HD,
    )
    head_loop(offset, load, store_into(qg_ref, kv_ref, sum_ref, add=False))


def kernel_cost(rows, keys, feats):
    heads = feats // HD
    return pl.CostEstimate(
        flops=heads * 12 * rows * keys * HD,
        transcendentals=heads * rows * keys,
        bytes_accessed=2 * feats * (3 * rows + 4 * keys),
    )


def kept_backward(stash, grads, offset, pick):
    _, keys, feats = stash.shape
    rows = grads.shape[1]
    bf16 = jnp.bfloat16
    out_shape = (
        jax.ShapeDtypeStruct((2, rows, feats), bf16),
        jax.ShapeDtypeStruct((2, 2, keys, feats), bf16),
        jax.ShapeDtypeStruct((3, feats), jnp.float32),
    )
    grid_spec = pltpu.PrefetchScalarGridSpec(
        num_scalar_prefetch=1,
        grid=(1,),
        in_specs=[
            pl.BlockSpec((3, keys, feats), lambda i, m: (0, 0, 0)),
            pl.BlockSpec((None, rows, feats), lambda i, m: (m[1], 0, 0)),
        ],
        out_specs=(
            pl.BlockSpec((None, rows, feats), lambda i, m: (0, 0, 0)),
            pl.BlockSpec((None, 2, keys, feats), lambda i, m: (0, 0, 0, 0)),
            pl.BlockSpec((3, feats), lambda i, m: (0, 0)),
        ),
    )
    meta = jnp.stack([offset, pick]).astype(jnp.int32)
    return pl.pallas_call(
        kept_kernel,
        out_shape=out_shape,
        grid_spec=grid_spec,
        cost_estimate=kernel_cost(rows, keys, feats),
        name="kept_backward",
    )(meta, stash, grads)


def held_backward(part, grads, offset, pick, chunk):
    rows = grads.shape[1]
    width = part.shape[1]
    keys = (part.shape[0] - rows) // 2
    bf16 = jnp.bfloat16
    grid_spec = pltpu.PrefetchScalarGridSpec(
        num_scalar_prefetch=1,
        grid=(1,),
        in_specs=[
            pl.BlockSpec((part.shape[0], width), lambda i, m: (0, 0)),
            pl.BlockSpec((None, rows, width), lambda i, m: (m[1], 0, chunk)),
        ],
        out_specs=(
            pl.BlockSpec((rows, width), lambda i, m: (0, 0)),
            pl.BlockSpec((2, keys, width), lambda i, m: (0, 0, 0)),
            pl.BlockSpec((3, width), lambda i, m: (0, 0)),
        ),
    )
    meta = jnp.stack([offset, 1 - pick]).astype(jnp.int32)
    return pl.pallas_call(
        held_kernel,
        out_shape=(
            jax.ShapeDtypeStruct((rows, width), bf16),
            jax.ShapeDtypeStruct((2, keys, width), bf16),
            jax.ShapeDtypeStruct((3, width), jnp.float32),
        ),
        grid_spec=grid_spec,
        cost_estimate=kernel_cost(rows, keys, width),
        name="held_backward",
    )(meta, part, grads)


def chunk_count(heads):
    for count in range(min(MAX_CHUNKS, heads), 0, -1):
        if heads % count == 0:
            return count
    return 1


def body(kept_qkv, held_qkv, sent_grad, order, offsets):
    section_count = lax.axis_size("pipe")
    half_way = section_count // 2
    section_index = lax.axis_index("pipe")
    feats = kept_qkv.shape[-1]
    keys = kept_qkv.shape[-2]
    heads = feats // HD

    owner = (section_index + section_count - half_way) % section_count
    owner_offset = lax.dynamic_index_in_dim(offsets[0], owner, 0, keepdims=False)[1]
    rows = sent_grad.shape[3] * lax.axis_size("tensor")
    held = held_qkv[0, 0]
    held_q = lax.dynamic_slice_in_dim(held[0], owner_offset, rows, 0)
    chunks = chunk_count(heads)
    width = feats // chunks
    fetched = []
    for c in range(chunks):
        cols = slice(c * width, (c + 1) * width)
        part = jnp.concatenate([held_q[:, cols], held[1, :, cols], held[2, :, cols]], axis=0)
        fetched.append(from_behind(part, "pipe", half_way))

    arrived = from_behind(sent_grad[0, 0], "pipe", -1)
    tensor_count = lax.axis_size("tensor")
    local_rows = arrived.shape[1]
    split = arrived.reshape(2, local_rows, tensor_count, feats).transpose(2, 0, 1, 3)
    regrouped = lax.all_to_all(split, "tensor", split_axis=0, concat_axis=0, tiled=True)
    regrouped = regrouped.transpose(1, 0, 2, 3).reshape(2, rows, feats)
    pick = order[0, 0]
    section_offsets = lax.dynamic_index_in_dim(offsets[0], section_index, 0, keepdims=False)
    qg, kv, column_sums = kept_backward(kept_qkv[0, 0], regrouped, section_offsets[0], pick)
    first_part, qg, kv, column_sums = lax.optimization_barrier((fetched[0], qg, kv, column_sums))
    fetched = [first_part] + fetched[1:]
    held_parts = [
        held_backward(fetched[c], regrouped, section_offsets[1], pick, c) for c in range(chunks)
    ]
    for c, (part_q, part_kv, _) in enumerate(held_parts):
        qg = lax.dynamic_update_slice(qg, part_q[None], (1, 0, c * width))
        kv = lax.dynamic_update_slice(kv, part_kv[None], (1, 0, 0, c * width))
    column_sums = column_sums + jnp.concatenate([part[2] for part in held_parts], axis=1)
    query_grad = qg
    key_value_grad = kv
    if lax.axis_size("dp") == 2:
        bias_grad = column_sums + from_behind(column_sums, "dp", 1)
    else:
        bias_grad = lax.psum(column_sums, "dp")
    return (query_grad[None, None], key_value_grad[None, None], bias_grad[None])


def solution(mesh):
    return jax.shard_map(
        body,
        mesh=mesh,
        in_specs=(
            P("dp", "pipe", None, None, "tensor"),
            P("dp", "pipe", None, None, "tensor"),
            P("dp", "pipe", None, "tensor", None),
            P("dp", "pipe"),
            P("dp", None, None),
        ),
        out_specs=(
            P("dp", "pipe", None, None, "tensor"),
            P("dp", "pipe", None, None, None, "tensor"),
            P("pipe", None, "tensor"),
        ),
        check_vma=False,
    )
```

```python
import functools
import math

import jax
import jax.numpy as jnp
from jax import lax
from jax.experimental import pallas as pl
from jax.experimental.pallas import tpu as pltpu
from jax.sharding import PartitionSpec as P

HD = 128
MASK_FILL = -1e30
MAX_CHUNKS = 4
NT_DIMS = (((1,), (1,)), ((), ()))


def from_behind(value, axis, steps):
    count = lax.axis_size(axis)
    pairs = [(source, (source + steps) % count) for source in range(count)]
    return lax.ppermute(value, axis, pairs)


def head_backward(q, k, v, g, visible):
    f32, bf16 = jnp.float32, jnp.bfloat16
    scale = 1.0 / math.sqrt(HD)
    s = lax.dot_general(q, k, NT_DIMS, preferred_element_type=f32) * scale
    s = jnp.where(visible, s, MASK_FILL)
    m = jnp.max(s, axis=1, keepdims=True)
    e = jnp.exp(s - m)
    p = e / jnp.sum(e, axis=1, keepdims=True)
    p_low = p.astype(bf16)
    ctx = jnp.dot(p_low, v, preferred_element_type=f32).astype(bf16)
    delta = jnp.sum(g.astype(f32) * ctx.astype(f32), axis=1, keepdims=True)
    dp = lax.dot_general(g, v, NT_DIMS, preferred_element_type=f32)
    ds = (p * (dp - delta) * scale).astype(bf16)
    dq = jnp.dot(ds, k, preferred_element_type=f32).astype(bf16)
    dk = jnp.dot(ds.T, q, preferred_element_type=f32).astype(bf16)
    dv = jnp.dot(p_low.T, g, preferred_element_type=f32).astype(bf16)
    return dq, dk, dv


def head_loop(offset, load, store):
    rows, keys, heads = load.rows, load.keys, load.heads
    pos = offset + lax.broadcasted_iota(jnp.int32, (rows, keys), 0)
    col = lax.broadcasted_iota(jnp.int32, (rows, keys), 1)
    visible = col <= pos

    def head(h, carry):
        cols = pl.ds(pl.multiple_of(h * HD, HD), HD)
        q, k, v, g = load(cols)
        store(cols, *head_backward(q, k, v, g, visible))
        return carry

    lax.fori_loop(0, heads, head, 0, unroll=True)


class Loader:
    def __init__(self, fn, rows, keys, heads):
        self.fn, self.rows, self.keys, self.heads = fn, rows, keys, heads

    def __call__(self, cols):
        return self.fn(cols)


def store_into(qg_ref, kv_ref, sum_ref, add, shift=0):
    f32 = jnp.float32

    def store(cols, dq, dk, dv):
        out = pl.ds(pl.multiple_of(cols.start + shift, HD), HD) if shift else cols
        qg_ref[:, out] = dq
        kv_ref[0, :, out] = dk
        kv_ref[1, :, out] = dv
        for row, value in enumerate((dq, dk, dv)):
            total = jnp.sum(value.astype(f32), axis=0, keepdims=True)
            if add:
                total = sum_ref[pl.ds(row, 1), out] + total
            sum_ref[pl.ds(row, 1), out] = total

    return store


def kept_kernel(meta_ref, x_ref, g_ref, qg_ref, kv_ref, sum_ref):
    offset = meta_ref[0]
    rows, feats = g_ref.shape
    keys = x_ref.shape[1]
    start = pl.multiple_of(offset, 16)
    load = Loader(
        lambda cols: (x_ref[0, pl.ds(start, rows), cols], x_ref[1, :, cols], x_ref[2, :, cols], g_ref[:, cols]),
        rows, keys, feats // HD,
    )
    head_loop(offset, load, store_into(qg_ref, kv_ref, sum_ref, add=False))


def held_kernel(meta_ref, x_ref, g_ref, qg_ref, kv_ref, sum_ref):
    offset = meta_ref[0]
    rows, feats = g_ref.shape
    keys = (x_ref.shape[0] - rows) // 2
    load = Loader(
        lambda cols: (x_ref[pl.ds(0, rows), cols], x_ref[pl.ds(rows, keys), cols],
                      x_ref[pl.ds(rows + keys, keys), cols], g_ref[:, cols]),
        rows, keys, feats // HD,
    )
    head_loop(offset, load, store_into(qg_ref, kv_ref, sum_ref, add=False))


def kernel_cost(rows, keys, feats):
    heads = feats // HD
    return pl.CostEstimate(
        flops=heads * 12 * rows * keys * HD,
        transcendentals=heads * rows * keys,
        bytes_accessed=2 * feats * (3 * rows + 4 * keys),
    )


def kept_backward(stash, grads, offset, pick):
    _, keys, feats = stash.shape
    rows = grads.shape[1]
    bf16 = jnp.bfloat16
    out_shape = (
        jax.ShapeDtypeStruct((2, rows, feats), bf16),
        jax.ShapeDtypeStruct((2, 2, keys, feats), bf16),
        jax.ShapeDtypeStruct((3, feats), jnp.float32),
    )
    grid_spec = pltpu.PrefetchScalarGridSpec(
        num_scalar_prefetch=1,
        grid=(1,),
        in_specs=[
            pl.BlockSpec((3, keys, feats), lambda i, m: (0, 0, 0)),
            pl.BlockSpec((None, rows, feats), lambda i, m: (m[1], 0, 0)),
        ],
        out_specs=(
            pl.BlockSpec((None, rows, feats), lambda i, m: (0, 0, 0)),
            pl.BlockSpec((None, 2, keys, feats), lambda i, m: (0, 0, 0, 0)),
            pl.BlockSpec((3, feats), lambda i, m: (0, 0)),
        ),
    )
    meta = jnp.stack([offset, pick]).astype(jnp.int32)
    return pl.pallas_call(
        kept_kernel,
        out_shape=out_shape,
        grid_spec=grid_spec,
        cost_estimate=kernel_cost(rows, keys, feats),
        name="kept_backward",
    )(meta, stash, grads)


def held_backward(part, grads, offset, pick, chunk):
    rows = grads.shape[1]
    width = part.shape[1]
    keys = (part.shape[0] - rows) // 2
    bf16 = jnp.bfloat16
    grid_spec = pltpu.PrefetchScalarGridSpec(
        num_scalar_prefetch=1,
        grid=(1,),
        in_specs=[
            pl.BlockSpec((part.shape[0], width), lambda i, m: (0, 0)),
            pl.BlockSpec((None, rows, width), lambda i, m: (m[1], 0, chunk)),
        ],
        out_specs=(
            pl.BlockSpec((rows, width), lambda i, m: (0, 0)),
            pl.BlockSpec((2, keys, width), lambda i, m: (0, 0, 0)),
            pl.BlockSpec((3, width), lambda i, m: (0, 0)),
        ),
    )
    meta = jnp.stack([offset, 1 - pick]).astype(jnp.int32)
    return pl.pallas_call(
        held_kernel,
        out_shape=(
            jax.ShapeDtypeStruct((rows, width), bf16),
            jax.ShapeDtypeStruct((2, keys, width), bf16),
            jax.ShapeDtypeStruct((3, width), jnp.float32),
        ),
        grid_spec=grid_spec,
        cost_estimate=kernel_cost(rows, keys, width),
        name="held_backward",
    )(meta, part, grads)


def held_last_kernel(count, meta_ref, x_ref, g_ref, *refs):
    prev_q, prev_kv = refs[:count], refs[count:2 * count]
    qg_ref, kv_ref, sum_ref = refs[2 * count + 2:]
    offset = meta_ref[0]
    rows, width = g_ref.shape
    keys = (x_ref.shape[0] - rows) // 2
    for c in range(count):
        cols = pl.ds(c * width, width)
        qg_ref[:, cols] = prev_q[c][...]
        kv_ref[:, :, cols] = prev_kv[c][...]
    load = Loader(
        lambda cols: (x_ref[pl.ds(0, rows), cols], x_ref[pl.ds(rows, keys), cols],
                      x_ref[pl.ds(rows + keys, keys), cols], g_ref[:, cols]),
        rows, keys, width // HD,
    )
    head_loop(offset, load, store_into(qg_ref, kv_ref, sum_ref, add=False, shift=count * width))


def held_last_backward(part, grads, offset, pick, chunk, earlier, qg, kv):
    rows = grads.shape[1]
    width = part.shape[1]
    keys = (part.shape[0] - rows) // 2
    feats = qg.shape[-1]
    count = len(earlier)
    vmem_q = pl.BlockSpec((rows, width), lambda i, m: (0, 0))
    vmem_kv = pl.BlockSpec((2, keys, width), lambda i, m: (0, 0, 0))
    grid_spec = pltpu.PrefetchScalarGridSpec(
        num_scalar_prefetch=1,
        grid=(1,),
        in_specs=[
            pl.BlockSpec((part.shape[0], width), lambda i, m: (0, 0)),
            pl.BlockSpec((None, rows, width), lambda i, m: (m[1], 0, chunk)),
        ] + [vmem_q] * count + [vmem_kv] * count + [
            pl.BlockSpec(memory_space=pl.ANY),
            pl.BlockSpec(memory_space=pl.ANY),
        ],
        out_specs=(
            pl.BlockSpec((None, rows, feats), lambda i, m: (1, 0, 0)),
            pl.BlockSpec((None, 2, keys, feats), lambda i, m: (1, 0, 0, 0)),
            pl.BlockSpec((3, feats), lambda i, m: (0, 0)),
        ),
    )
    meta = jnp.stack([offset, 1 - pick]).astype(jnp.int32)
    first_alias = 2 + 2 * count + 1
    return pl.pallas_call(
        functools.partial(held_last_kernel, count),
        out_shape=(
            jax.ShapeDtypeStruct(qg.shape, qg.dtype),
            jax.ShapeDtypeStruct(kv.shape, kv.dtype),
            jax.ShapeDtypeStruct((3, feats), jnp.float32),
        ),
        grid_spec=grid_spec,
        input_output_aliases={first_alias: 0, first_alias + 1: 1},
        cost_estimate=kernel_cost(rows, keys, width),
        name="held_last_backward",
    )(meta, part, grads, *[e[0] for e in earlier], *[e[1] for e in earlier], qg, kv)


def chunk_count(heads):
    for count in range(min(MAX_CHUNKS, heads), 0, -1):
        if heads % count == 0:
            return count
    return 1


def body(kept_qkv, held_qkv, sent_grad, order, offsets):
    section_count = lax.axis_size("pipe")
    half_way = section_count // 2
    section_index = lax.axis_index("pipe")
    feats = kept_qkv.shape[-1]
    keys = kept_qkv.shape[-2]
    heads = feats // HD

    owner = (section_index + section_count - half_way) % section_count
    owner_offset = lax.dynamic_index_in_dim(offsets[0], owner, 0, keepdims=False)[1]
    rows = sent_grad.shape[3] * lax.axis_size("tensor")
    held = held_qkv[0, 0]
    held_q = lax.dynamic_slice_in_dim(held[0], owner_offset, rows, 0)
    chunks = chunk_count(heads)
    width = feats // chunks
    fetched = []
    for c in range(chunks):
        cols = slice(c * width, (c + 1) * width)
        part = jnp.concatenate([held_q[:, cols], held[1, :, cols], held[2, :, cols]], axis=0)
        fetched.append(from_behind(part, "pipe", half_way))

    arrived = from_behind(sent_grad[0, 0], "pipe", -1)
    tensor_count = lax.axis_size("tensor")
    local_rows = arrived.shape[1]
    split = arrived.reshape(2, local_rows, tensor_count, feats).transpose(2, 0, 1, 3)
    regrouped = lax.all_to_all(split, "tensor", split_axis=0, concat_axis=0, tiled=True)
    regrouped = regrouped.transpose(1, 0, 2, 3).reshape(2, rows, feats)
    pick = order[0, 0]
    section_offsets = lax.dynamic_index_in_dim(offsets[0], section_index, 0, keepdims=False)
    qg, kv, column_sums = kept_backward(kept_qkv[0, 0], regrouped, section_offsets[0], pick)
    first_part, qg, kv, column_sums = lax.optimization_barrier((fetched[0], qg, kv, column_sums))
    fetched = [first_part] + fetched[1:]
    held_parts = [
        held_backward(fetched[c], regrouped, section_offsets[1], pick, c) for c in range(chunks - 1)
    ]
    qg, kv, last_sums = held_last_backward(
        fetched[-1], regrouped, section_offsets[1], pick, chunks - 1, held_parts, qg, kv
    )
    last_sums = last_sums[:, (chunks - 1) * width:]
    column_sums = column_sums + jnp.concatenate([part[2] for part in held_parts] + [last_sums], axis=1)
    query_grad = qg
    key_value_grad = kv
    if lax.axis_size("dp") == 2:
        bias_grad = column_sums + from_behind(column_sums, "dp", 1)
    else:
        bias_grad = lax.psum(column_sums, "dp")
    return (query_grad[None, None], key_value_grad[None, None], bias_grad[None])


def solution(mesh):
    return jax.shard_map(
        body,
        mesh=mesh,
        in_specs=(
            P("dp", "pipe", None, None, "tensor"),
            P("dp", "pipe", None, None, "tensor"),
            P("dp", "pipe", None, "tensor", None),
            P("dp", "pipe"),
            P("dp", None, None),
        ),
        out_specs=(
            P("dp", "pipe", None, None, "tensor"),
            P("dp", "pipe", None, None, None, "tensor"),
            P("pipe", None, "tensor"),
        ),
        check_vma=False,
    )
```

```python
import functools
import math

import jax
import jax.numpy as jnp
from jax import lax
from jax.experimental import pallas as pl
from jax.experimental.pallas import tpu as pltpu
from jax.sharding import PartitionSpec as P

HD = 128
MASK_FILL = -1e30
MAX_CHUNKS = 4
NT_DIMS = (((1,), (1,)), ((), ()))


def from_behind(value, axis, steps):
    count = lax.axis_size(axis)
    pairs = [(source, (source + steps) % count) for source in range(count)]
    return lax.ppermute(value, axis, pairs)


def head_backward(q, k, v, g, visible):
    f32, bf16 = jnp.float32, jnp.bfloat16
    scale = 1.0 / math.sqrt(HD)
    s = lax.dot_general(q, k, NT_DIMS, preferred_element_type=f32) * scale
    s = jnp.where(visible, s, MASK_FILL)
    m = jnp.max(s, axis=1, keepdims=True)
    e = jnp.exp(s - m)
    p = e / jnp.sum(e, axis=1, keepdims=True)
    p_low = p.astype(bf16)
    ctx = jnp.dot(p_low, v, preferred_element_type=f32).astype(bf16)
    delta = jnp.sum(g.astype(f32) * ctx.astype(f32), axis=1, keepdims=True)
    dp = lax.dot_general(g, v, NT_DIMS, preferred_element_type=f32)
    ds = (p * (dp - delta) * scale).astype(bf16)
    dq = jnp.dot(ds, k, preferred_element_type=f32).astype(bf16)
    dk = jnp.dot(ds.T, q, preferred_element_type=f32).astype(bf16)
    dv = jnp.dot(p_low.T, g, preferred_element_type=f32).astype(bf16)
    return dq, dk, dv


def head_loop(offset, load, store):
    rows, keys, heads = load.rows, load.keys, load.heads
    pos = offset + lax.broadcasted_iota(jnp.int32, (rows, keys), 0)
    col = lax.broadcasted_iota(jnp.int32, (rows, keys), 1)
    visible = col <= pos

    def head(h, carry):
        cols = pl.ds(pl.multiple_of(h * HD, HD), HD)
        q, k, v, g = load(cols)
        store(cols, *head_backward(q, k, v, g, visible))
        return carry

    lax.fori_loop(0, heads, head, 0, unroll=True)


class Loader:
    def __init__(self, fn, rows, keys, heads):
        self.fn, self.rows, self.keys, self.heads = fn, rows, keys, heads

    def __call__(self, cols):
        return self.fn(cols)


def store_into(qg_ref, kv_ref, sum_ref, add):
    f32 = jnp.float32

    def store(cols, dq, dk, dv):
        qg_ref[:, cols] = dq
        kv_ref[0, :, cols] = dk
        kv_ref[1, :, cols] = dv
        for row, value in enumerate((dq, dk, dv)):
            total = jnp.sum(value.astype(f32), axis=0, keepdims=True)
            if add:
                total = sum_ref[pl.ds(row, 1), cols] + total
            sum_ref[pl.ds(row, 1), cols] = total

    return store


def kept_kernel(meta_ref, x_ref, g_ref, qg_ref, kv_ref, sum_ref):
    offset = meta_ref[0]
    rows, feats = g_ref.shape
    keys = x_ref.shape[1]
    start = pl.multiple_of(offset, 16)
    load = Loader(
        lambda cols: (x_ref[0, pl.ds(start, rows), cols], x_ref[1, :, cols], x_ref[2, :, cols], g_ref[:, cols]),
        rows, keys, feats // HD,
    )
    head_loop(offset, load, store_into(qg_ref, kv_ref, sum_ref, add=False))


def held_kernel(meta_ref, x_ref, g_ref, qg_ref, kv_ref, sum_ref):
    offset = meta_ref[0]
    rows, feats = g_ref.shape
    keys = (x_ref.shape[0] - rows) // 2
    load = Loader(
        lambda cols: (x_ref[pl.ds(0, rows), cols], x_ref[pl.ds(rows, keys), cols],
                      x_ref[pl.ds(rows + keys, keys), cols], g_ref[:, cols]),
        rows, keys, feats // HD,
    )
    head_loop(offset, load, store_into(qg_ref, kv_ref, sum_ref, add=False))


def kernel_cost(rows, keys, feats):
    heads = feats // HD
    return pl.CostEstimate(
        flops=heads * 12 * rows * keys * HD,
        transcendentals=heads * rows * keys,
        bytes_accessed=2 * feats * (3 * rows + 4 * keys),
    )


def kept_backward(stash, grads, offset, pick):
    _, keys, feats = stash.shape
    rows = grads.shape[1]
    bf16 = jnp.bfloat16
    out_shape = (
        jax.ShapeDtypeStruct((2, rows, feats), bf16),
        jax.ShapeDtypeStruct((2, 2, keys, feats), bf16),
        jax.ShapeDtypeStruct((3, feats), jnp.float32),
    )
    grid_spec = pltpu.PrefetchScalarGridSpec(
        num_scalar_prefetch=1,
        grid=(1,),
        in_specs=[
            pl.BlockSpec((3, keys, feats), lambda i, m: (0, 0, 0)),
            pl.BlockSpec((None, rows, feats), lambda i, m: (m[1], 0, 0)),
        ],
        out_specs=(
            pl.BlockSpec((None, rows, feats), lambda i, m: (0, 0, 0)),
            pl.BlockSpec((None, 2, keys, feats), lambda i, m: (0, 0, 0, 0)),
            pl.BlockSpec((3, feats), lambda i, m: (0, 0)),
        ),
    )
    meta = jnp.stack([offset, pick]).astype(jnp.int32)
    return pl.pallas_call(
        kept_kernel,
        out_shape=out_shape,
        grid_spec=grid_spec,
        cost_estimate=kernel_cost(rows, keys, feats),
        name="kept_backward",
    )(meta, stash, grads)


def held_backward(part, grads, offset, pick, lo):
    rows = grads.shape[1]
    width = part.shape[1]
    assert lo % width == 0
    chunk = lo // width
    keys = (part.shape[0] - rows) // 2
    bf16 = jnp.bfloat16
    grid_spec = pltpu.PrefetchScalarGridSpec(
        num_scalar_prefetch=1,
        grid=(1,),
        in_specs=[
            pl.BlockSpec((part.shape[0], width), lambda i, m: (0, 0)),
            pl.BlockSpec((None, rows, width), lambda i, m: (m[1], 0, chunk)),
        ],
        out_specs=(
            pl.BlockSpec((rows, width), lambda i, m: (0, 0)),
            pl.BlockSpec((2, keys, width), lambda i, m: (0, 0, 0)),
            pl.BlockSpec((3, width), lambda i, m: (0, 0)),
        ),
    )
    meta = jnp.stack([offset, 1 - pick]).astype(jnp.int32)
    return pl.pallas_call(
        held_kernel,
        out_shape=(
            jax.ShapeDtypeStruct((rows, width), bf16),
            jax.ShapeDtypeStruct((2, keys, width), bf16),
            jax.ShapeDtypeStruct((3, width), jnp.float32),
        ),
        grid_spec=grid_spec,
        cost_estimate=kernel_cost(rows, keys, width),
        name="held_backward",
    )(meta, part, grads)


def assemble_kernel(bounds, *refs):
    count = len(bounds)
    q_parts, kv_parts, sum_parts = refs[:count], refs[count:2 * count], refs[2 * count:3 * count]
    kept_sums = refs[3 * count]
    qg_ref, kv_ref, sum_ref = refs[3 * count + 3:]
    for c, (lo, hi) in enumerate(bounds):
        qg_ref[:, lo:hi] = q_parts[c][...]
        kv_ref[:, :, lo:hi] = kv_parts[c][...]
        sum_ref[:, lo:hi] = kept_sums[:, lo:hi] + sum_parts[c][...]


def assemble(bounds, held_parts, kept_sums, qg, kv):
    rows, feats = qg.shape[1], qg.shape[2]
    keys = kv.shape[2]
    whole = lambda shape: pl.BlockSpec(shape, lambda i: (0,) * len(shape))
    in_specs = (
        [whole(part[0].shape) for part in held_parts]
        + [whole(part[1].shape) for part in held_parts]
        + [whole(part[2].shape) for part in held_parts]
        + [whole(kept_sums.shape), pl.BlockSpec(memory_space=pl.ANY), pl.BlockSpec(memory_space=pl.ANY)]
    )
    count = len(held_parts)
    first_alias = 3 * count + 1
    return pl.pallas_call(
        functools.partial(assemble_kernel, tuple(bounds)),
        out_shape=(
            jax.ShapeDtypeStruct(qg.shape, qg.dtype),
            jax.ShapeDtypeStruct(kv.shape, kv.dtype),
            jax.ShapeDtypeStruct(kept_sums.shape, kept_sums.dtype),
        ),
        grid=(1,),
        in_specs=in_specs,
        out_specs=(
            pl.BlockSpec((None, rows, feats), lambda i: (1, 0, 0)),
            pl.BlockSpec((None, 2, keys, feats), lambda i: (1, 0, 0, 0)),
            whole(kept_sums.shape),
        ),
        input_output_aliases={first_alias: 0, first_alias + 1: 1},
        cost_estimate=pl.CostEstimate(flops=0, transcendentals=0, bytes_accessed=4 * 2 * feats * (rows + 2 * keys)),
        name="assemble_held",
    )(*[p[0] for p in held_parts], *[p[1] for p in held_parts], *[p[2] for p in held_parts], kept_sums, qg, kv)


def chunk_bounds(heads):
    sizes = [heads // 3, heads // 3, heads // 6]
    sizes.append(heads - sum(sizes))
    if min(sizes) < 1:
        sizes = [heads]
    bounds, lo = [], 0
    for size in sizes:
        if lo % size:
            return [(c * HD, (c + 1) * HD) for c in range(heads)] if heads <= 4 else chunk_bounds_even(heads)
        bounds.append((lo * HD, (lo + size) * HD))
        lo += size
    return bounds


def chunk_bounds_even(heads):
    count = next(n for n in (4, 3, 2, 1) if heads % n == 0)
    size = heads // count
    return [(c * size * HD, (c + 1) * size * HD) for c in range(count)]


def chunk_count(heads):
    for count in range(min(MAX_CHUNKS, heads), 0, -1):
        if heads % count == 0:
            return count
    return 1


def body(kept_qkv, held_qkv, sent_grad, order, offsets):
    section_count = lax.axis_size("pipe")
    half_way = section_count // 2
    section_index = lax.axis_index("pipe")
    feats = kept_qkv.shape[-1]
    keys = kept_qkv.shape[-2]
    heads = feats // HD

    owner = (section_index + section_count - half_way) % section_count
    owner_offset = lax.dynamic_index_in_dim(offsets[0], owner, 0, keepdims=False)[1]
    rows = sent_grad.shape[3] * lax.axis_size("tensor")
    held = held_qkv[0, 0]
    held_q = lax.dynamic_slice_in_dim(held[0], owner_offset, rows, 0)
    bounds = chunk_bounds_even(heads)
    fetched = []
    for lo, hi in bounds:
        part = jnp.concatenate([held_q[:, lo:hi], held[1, :, lo:hi], held[2, :, lo:hi]], axis=0)
        fetched.append(from_behind(part, "pipe", half_way))

    arrived = from_behind(sent_grad[0, 0], "pipe", -1)
    tensor_count = lax.axis_size("tensor")
    local_rows = arrived.shape[1]
    split = arrived.reshape(2, local_rows, tensor_count, feats).transpose(2, 0, 1, 3)
    regrouped = lax.all_to_all(split, "tensor", split_axis=0, concat_axis=0, tiled=True)
    regrouped = regrouped.transpose(1, 0, 2, 3).reshape(2, rows, feats)
    pick = order[0, 0]
    section_offsets = lax.dynamic_index_in_dim(offsets[0], section_index, 0, keepdims=False)
    qg, kv, column_sums = kept_backward(kept_qkv[0, 0], regrouped, section_offsets[0], pick)
    first_part, qg, kv, column_sums = lax.optimization_barrier((fetched[0], qg, kv, column_sums))
    fetched = [first_part] + fetched[1:]
    first_part, qg, kv, column_sums = lax.optimization_barrier((fetched[0], qg, kv, column_sums))
    fetched = [first_part] + fetched[1:]
    held_parts = [
        held_backward(part, regrouped, section_offsets[1], pick, lo)
        for (lo, _), part in zip(bounds, fetched)
    ]
    qg, kv, column_sums = assemble(bounds, held_parts, column_sums, qg, kv)
    query_grad = qg
    key_value_grad = kv
    if lax.axis_size("dp") == 2:
        bias_grad = column_sums + from_behind(column_sums, "dp", 1)
    else:
        bias_grad = lax.psum(column_sums, "dp")
    return (query_grad[None, None], key_value_grad[None, None], bias_grad[None])


def solution(mesh):
    return jax.shard_map(
        body,
        mesh=mesh,
        in_specs=(
            P("dp", "pipe", None, None, "tensor"),
            P("dp", "pipe", None, None, "tensor"),
            P("dp", "pipe", None, "tensor", None),
            P("dp", "pipe"),
            P("dp", None, None),
        ),
        out_specs=(
            P("dp", "pipe", None, None, "tensor"),
            P("dp", "pipe", None, None, None, "tensor"),
            P("pipe", None, "tensor"),
        ),
        check_vma=False,
    )
```

```python
import functools
import math

import jax
import jax.numpy as jnp
from jax import lax
from jax.experimental import pallas as pl
from jax.experimental.pallas import tpu as pltpu
from jax.sharding import PartitionSpec as P

HD = 128
MASK_FILL = -1e30
MAX_CHUNKS = 4
NT_DIMS = (((1,), (1,)), ((), ()))


def from_behind(value, axis, steps):
    count = lax.axis_size(axis)
    pairs = [(source, (source + steps) % count) for source in range(count)]
    return lax.ppermute(value, axis, pairs)


def head_backward(q, k, v, g, visible):
    f32, bf16 = jnp.float32, jnp.bfloat16
    scale = 1.0 / math.sqrt(HD)
    s = lax.dot_general(q, k, NT_DIMS, preferred_element_type=f32) * scale
    s = jnp.where(visible, s, MASK_FILL)
    m = jnp.max(s, axis=1, keepdims=True)
    e = jnp.exp(s - m)
    p = e / jnp.sum(e, axis=1, keepdims=True)
    p_low = p.astype(bf16)
    ctx = jnp.dot(p_low, v, preferred_element_type=f32).astype(bf16)
    delta = jnp.sum(g.astype(f32) * ctx.astype(f32), axis=1, keepdims=True)
    dp = lax.dot_general(g, v, NT_DIMS, preferred_element_type=f32)
    ds = (p * (dp - delta) * scale).astype(bf16)
    dq = jnp.dot(ds, k, preferred_element_type=f32).astype(bf16)
    dk = jnp.dot(ds.T, q, preferred_element_type=f32).astype(bf16)
    dv = jnp.dot(p_low.T, g, preferred_element_type=f32).astype(bf16)
    return dq, dk, dv


def head_loop(offset, load, store):
    rows, keys, heads = load.rows, load.keys, load.heads
    pos = offset + lax.broadcasted_iota(jnp.int32, (rows, keys), 0)
    col = lax.broadcasted_iota(jnp.int32, (rows, keys), 1)
    visible = col <= pos

    def head(h, carry):
        cols = pl.ds(pl.multiple_of(h * HD, HD), HD)
        q, k, v, g = load(cols)
        store(cols, *head_backward(q, k, v, g, visible))
        return carry

    lax.fori_loop(0, heads, head, 0, unroll=True)


class Loader:
    def __init__(self, fn, rows, keys, heads):
        self.fn, self.rows, self.keys, self.heads = fn, rows, keys, heads

    def __call__(self, cols):
        return self.fn(cols)


def store_into(qg_ref, kv_ref, sum_ref, add):
    f32 = jnp.float32

    def store(cols, dq, dk, dv):
        qg_ref[:, cols] = dq
        kv_ref[0, :, cols] = dk
        kv_ref[1, :, cols] = dv
        for row, value in enumerate((dq, dk, dv)):
            total = jnp.sum(value.astype(f32), axis=0, keepdims=True)
            if add:
                total = sum_ref[pl.ds(row, 1), cols] + total
            sum_ref[pl.ds(row, 1), cols] = total

    return store


def kept_kernel(meta_ref, x_ref, g_ref, qg_ref, kv_ref, sum_ref):
    offset = meta_ref[0]
    rows, feats = g_ref.shape
    keys = x_ref.shape[1]
    start = pl.multiple_of(offset, 16)
    load = Loader(
        lambda cols: (x_ref[0, pl.ds(start, rows), cols], x_ref[1, :, cols], x_ref[2, :, cols], g_ref[:, cols]),
        rows, keys, feats // HD,
    )
    head_loop(offset, load, store_into(qg_ref, kv_ref, sum_ref, add=False))


def held_kernel(meta_ref, x_ref, g_ref, qg_ref, kv_ref, sum_ref):
    offset = meta_ref[0]
    rows, feats = g_ref.shape
    keys = (x_ref.shape[0] - rows) // 2
    load = Loader(
        lambda cols: (x_ref[pl.ds(0, rows), cols], x_ref[pl.ds(rows, keys), cols],
                      x_ref[pl.ds(rows + keys, keys), cols], g_ref[:, cols]),
        rows, keys, feats // HD,
    )
    head_loop(offset, load, store_into(qg_ref, kv_ref, sum_ref, add=False))


def kernel_cost(rows, keys, feats):
    heads = feats // HD
    return pl.CostEstimate(
        flops=heads * 12 * rows * keys * HD,
        transcendentals=heads * rows * keys,
        bytes_accessed=2 * feats * (3 * rows + 4 * keys),
    )


def kept_backward(stash, grads, offset, pick):
    _, keys, feats = stash.shape
    rows = grads.shape[1]
    bf16 = jnp.bfloat16
    out_shape = (
        jax.ShapeDtypeStruct((2, rows, feats), bf16),
        jax.ShapeDtypeStruct((2, 2, keys, feats), bf16),
        jax.ShapeDtypeStruct((3, feats), jnp.float32),
    )
    grid_spec = pltpu.PrefetchScalarGridSpec(
        num_scalar_prefetch=1,
        grid=(1,),
        in_specs=[
            pl.BlockSpec((3, keys, feats), lambda i, m: (0, 0, 0)),
            pl.BlockSpec((None, rows, feats), lambda i, m: (m[1], 0, 0)),
        ],
        out_specs=(
            pl.BlockSpec((None, rows, feats), lambda i, m: (0, 0, 0)),
            pl.BlockSpec((None, 2, keys, feats), lambda i, m: (0, 0, 0, 0)),
            pl.BlockSpec((3, feats), lambda i, m: (0, 0)),
        ),
    )
    meta = jnp.stack([offset, pick]).astype(jnp.int32)
    return pl.pallas_call(
        kept_kernel,
        out_shape=out_shape,
        grid_spec=grid_spec,
        cost_estimate=kernel_cost(rows, keys, feats),
        name="kept_backward",
    )(meta, stash, grads)


def held_backward(part, grads, offset, pick, lo):
    rows = grads.shape[1]
    width = part.shape[1]
    assert lo % width == 0
    chunk = lo // width
    keys = (part.shape[0] - rows) // 2
    bf16 = jnp.bfloat16
    grid_spec = pltpu.PrefetchScalarGridSpec(
        num_scalar_prefetch=1,
        grid=(1,),
        in_specs=[
            pl.BlockSpec((part.shape[0], width), lambda i, m: (0, 0)),
            pl.BlockSpec((None, rows, width), lambda i, m: (m[1], 0, chunk)),
        ],
        out_specs=(
            pl.BlockSpec((rows, width), lambda i, m: (0, 0)),
            pl.BlockSpec((2, keys, width), lambda i, m: (0, 0, 0)),
            pl.BlockSpec((3, width), lambda i, m: (0, 0)),
        ),
    )
    meta = jnp.stack([offset, 1 - pick]).astype(jnp.int32)
    return pl.pallas_call(
        held_kernel,
        out_shape=(
            jax.ShapeDtypeStruct((rows, width), bf16),
            jax.ShapeDtypeStruct((2, keys, width), bf16),
            jax.ShapeDtypeStruct((3, width), jnp.float32),
        ),
        grid_spec=grid_spec,
        cost_estimate=kernel_cost(rows, keys, width),
        name="held_backward",
    )(meta, part, grads)


def pack_kernel(count, half, bounds, off_ref, x_ref, *out_refs):
    owner = (lax.axis_index("pipe") + count - half) % count
    start = pl.multiple_of(off_ref[owner, 1], 16)
    rows = out_refs[0].shape[0] - 2 * x_ref.shape[1]
    keys = x_ref.shape[1]
    for (lo, hi), out_ref in zip(bounds, out_refs):
        out_ref[pl.ds(0, rows), :] = x_ref[0, pl.ds(start, rows), lo:hi]
        out_ref[pl.ds(rows, keys), :] = x_ref[1, :, lo:hi]
        out_ref[pl.ds(rows + keys, keys), :] = x_ref[2, :, lo:hi]


def pack_held(held, offsets, rows, count, half, bounds):
    keys = held.shape[1]
    out_shape = tuple(
        jax.ShapeDtypeStruct((rows + 2 * keys, hi - lo), held.dtype) for lo, hi in bounds
    )
    vmem = pl.BlockSpec(memory_space=pltpu.VMEM)
    return pl.pallas_call(
        functools.partial(pack_kernel, count, half, tuple(bounds)),
        out_shape=out_shape,
        in_specs=[pl.BlockSpec(memory_space=pltpu.SMEM), vmem],
        out_specs=tuple(vmem for _ in bounds),
        cost_estimate=pl.CostEstimate(flops=0, transcendentals=0, bytes_accessed=4 * held.size),
        name="pack_held",
    )(offsets, held)


def assemble_kernel(bounds, *refs):
    count = len(bounds)
    q_parts, kv_parts, sum_parts = refs[:count], refs[count:2 * count], refs[2 * count:3 * count]
    kept_sums = refs[3 * count]
    qg_ref, kv_ref, sum_ref = refs[3 * count + 3:]
    for c, (lo, hi) in enumerate(bounds):
        qg_ref[:, lo:hi] = q_parts[c][...]
        kv_ref[:, :, lo:hi] = kv_parts[c][...]
        sum_ref[:, lo:hi] = kept_sums[:, lo:hi] + sum_parts[c][...]


def assemble(bounds, held_parts, kept_sums, qg, kv):
    rows, feats = qg.shape[1], qg.shape[2]
    keys = kv.shape[2]
    whole = lambda shape: pl.BlockSpec(shape, lambda i: (0,) * len(shape))
    in_specs = (
        [whole(part[0].shape) for part in held_parts]
        + [whole(part[1].shape) for part in held_parts]
        + [whole(part[2].shape) for part in held_parts]
        + [whole(kept_sums.shape), pl.BlockSpec(memory_space=pl.ANY), pl.BlockSpec(memory_space=pl.ANY)]
    )
    count = len(held_parts)
    first_alias = 3 * count + 1
    return pl.pallas_call(
        functools.partial(assemble_kernel, tuple(bounds)),
        out_shape=(
            jax.ShapeDtypeStruct(qg.shape, qg.dtype),
            jax.ShapeDtypeStruct(kv.shape, kv.dtype),
            jax.ShapeDtypeStruct(kept_sums.shape, kept_sums.dtype),
        ),
        grid=(1,),
        in_specs=in_specs,
        out_specs=(
            pl.BlockSpec((None, rows, feats), lambda i: (1, 0, 0)),
            pl.BlockSpec((None, 2, keys, feats), lambda i: (1, 0, 0, 0)),
            whole(kept_sums.shape),
        ),
        input_output_aliases={first_alias: 0, first_alias + 1: 1},
        cost_estimate=pl.CostEstimate(flops=0, transcendentals=0, bytes_accessed=4 * 2 * feats * (rows + 2 * keys)),
        name="assemble_held",
    )(*[p[0] for p in held_parts], *[p[1] for p in held_parts], *[p[2] for p in held_parts], kept_sums, qg, kv)


def chunk_bounds(heads):
    sizes = [heads // 3, heads // 3, heads // 6]
    sizes.append(heads - sum(sizes))
    if min(sizes) < 1:
        sizes = [heads]
    bounds, lo = [], 0
    for size in sizes:
        if lo % size:
            return [(c * HD, (c + 1) * HD) for c in range(heads)] if heads <= 4 else chunk_bounds_even(heads)
        bounds.append((lo * HD, (lo + size) * HD))
        lo += size
    return bounds


def chunk_bounds_even(heads):
    count = next(n for n in (4, 3, 2, 1) if heads % n == 0)
    size = heads // count
    return [(c * size * HD, (c + 1) * size * HD) for c in range(count)]


def chunk_count(heads):
    for count in range(min(MAX_CHUNKS, heads), 0, -1):
        if heads % count == 0:
            return count
    return 1


def body(kept_qkv, held_qkv, sent_grad, order, offsets):
    section_count = lax.axis_size("pipe")
    half_way = section_count // 2
    section_index = lax.axis_index("pipe")
    feats = kept_qkv.shape[-1]
    keys = kept_qkv.shape[-2]
    heads = feats // HD

    rows = sent_grad.shape[3] * lax.axis_size("tensor")
    bounds = chunk_bounds_even(heads)
    parts = pack_held(held_qkv[0, 0], offsets[0], rows, section_count, half_way, bounds)
    fetched = [from_behind(part, "pipe", half_way) for part in parts]

    arrived = from_behind(sent_grad[0, 0], "pipe", -1)
    tensor_count = lax.axis_size("tensor")
    local_rows = arrived.shape[1]
    split = arrived.reshape(2, local_rows, tensor_count, feats).transpose(2, 0, 1, 3)
    regrouped = lax.all_to_all(split, "tensor", split_axis=0, concat_axis=0, tiled=True)
    regrouped = regrouped.transpose(1, 0, 2, 3).reshape(2, rows, feats)
    pick = order[0, 0]
    section_offsets = lax.dynamic_index_in_dim(offsets[0], section_index, 0, keepdims=False)
    qg, kv, column_sums = kept_backward(kept_qkv[0, 0], regrouped, section_offsets[0], pick)
    first_part, qg, kv, column_sums = lax.optimization_barrier((fetched[0], qg, kv, column_sums))
    fetched = [first_part] + fetched[1:]
    first_part, qg, kv, column_sums = lax.optimization_barrier((fetched[0], qg, kv, column_sums))
    fetched = [first_part] + fetched[1:]
    held_parts = [
        held_backward(part, regrouped, section_offsets[1], pick, lo)
        for (lo, _), part in zip(bounds, fetched)
    ]
    qg, kv, column_sums = assemble(bounds, held_parts, column_sums, qg, kv)
    query_grad = qg
    key_value_grad = kv
    if lax.axis_size("dp") == 2:
        bias_grad = column_sums + from_behind(column_sums, "dp", 1)
    else:
        bias_grad = lax.psum(column_sums, "dp")
    return (query_grad[None, None], key_value_grad[None, None], bias_grad[None])


def solution(mesh):
    return jax.shard_map(
        body,
        mesh=mesh,
        in_specs=(
            P("dp", "pipe", None, None, "tensor"),
            P("dp", "pipe", None, None, "tensor"),
            P("dp", "pipe", None, "tensor", None),
            P("dp", "pipe"),
            P("dp", None, None),
        ),
        out_specs=(
            P("dp", "pipe", None, None, "tensor"),
            P("dp", "pipe", None, None, None, "tensor"),
            P("pipe", None, "tensor"),
        ),
        check_vma=False,
    )
```

```python
import functools
import math

import jax
import jax.numpy as jnp
from jax import lax
from jax.experimental import pallas as pl
from jax.experimental.pallas import tpu as pltpu
from jax.sharding import PartitionSpec as P

HD = 128
MASK_FILL = -1e30
MAX_CHUNKS = 4
NT_DIMS = (((1,), (1,)), ((), ()))


def from_behind(value, axis, steps):
    count = lax.axis_size(axis)
    pairs = [(source, (source + steps) % count) for source in range(count)]
    return lax.ppermute(value, axis, pairs)


def head_backward(q, k, v, g, visible):
    f32, bf16 = jnp.float32, jnp.bfloat16
    scale = 1.0 / math.sqrt(HD)
    s = lax.dot_general(q, k, NT_DIMS, preferred_element_type=f32) * scale
    s = jnp.where(visible, s, MASK_FILL)
    m = jnp.max(s, axis=1, keepdims=True)
    e = jnp.exp(s - m)
    p = e / jnp.sum(e, axis=1, keepdims=True)
    p_low = p.astype(bf16)
    ctx = jnp.dot(p_low, v, preferred_element_type=f32).astype(bf16)
    delta = jnp.sum(g.astype(f32) * ctx.astype(f32), axis=1, keepdims=True)
    dp = lax.dot_general(g, v, NT_DIMS, preferred_element_type=f32)
    ds = (p * (dp - delta) * scale).astype(bf16)
    dq = jnp.dot(ds, k, preferred_element_type=f32).astype(bf16)
    dk = jnp.dot(ds.T, q, preferred_element_type=f32).astype(bf16)
    dv = jnp.dot(p_low.T, g, preferred_element_type=f32).astype(bf16)
    return dq, dk, dv


def head_loop(offset, load, store):
    rows, keys, heads = load.rows, load.keys, load.heads
    pos = offset + lax.broadcasted_iota(jnp.int32, (rows, keys), 0)
    col = lax.broadcasted_iota(jnp.int32, (rows, keys), 1)
    visible = col <= pos

    def head(h, carry):
        cols = pl.ds(pl.multiple_of(h * HD, HD), HD)
        q, k, v, g = load(cols)
        store(cols, *head_backward(q, k, v, g, visible))
        return carry

    lax.fori_loop(0, heads, head, 0, unroll=True)


class Loader:
    def __init__(self, fn, rows, keys, heads):
        self.fn, self.rows, self.keys, self.heads = fn, rows, keys, heads

    def __call__(self, cols):
        return self.fn(cols)


def store_into(qg_ref, kv_ref, sum_ref, add):
    f32 = jnp.float32

    def store(cols, dq, dk, dv):
        qg_ref[:, cols] = dq
        kv_ref[0, :, cols] = dk
        kv_ref[1, :, cols] = dv
        for row, value in enumerate((dq, dk, dv)):
            total = jnp.sum(value.astype(f32), axis=0, keepdims=True)
            if add:
                total = sum_ref[pl.ds(row, 1), cols] + total
            sum_ref[pl.ds(row, 1), cols] = total

    return store


def kept_kernel(meta_ref, x_ref, g_ref, qg_ref, kv_ref, sum_ref):
    offset = meta_ref[0]
    rows, feats = g_ref.shape
    keys = x_ref.shape[1]
    start = pl.multiple_of(offset, 16)
    load = Loader(
        lambda cols: (x_ref[0, pl.ds(start, rows), cols], x_ref[1, :, cols], x_ref[2, :, cols], g_ref[:, cols]),
        rows, keys, feats // HD,
    )
    head_loop(offset, load, store_into(qg_ref, kv_ref, sum_ref, add=False))


def held_kernel(meta_ref, x_ref, g_ref, qg_ref, kv_ref, sum_ref):
    offset = meta_ref[0]
    rows, feats = g_ref.shape
    keys = (x_ref.shape[0] - rows) // 2
    load = Loader(
        lambda cols: (x_ref[pl.ds(0, rows), cols], x_ref[pl.ds(rows, keys), cols],
                      x_ref[pl.ds(rows + keys, keys), cols], g_ref[:, cols]),
        rows, keys, feats // HD,
    )
    head_loop(offset, load, store_into(qg_ref, kv_ref, sum_ref, add=False))


def kernel_cost(rows, keys, feats):
    heads = feats // HD
    return pl.CostEstimate(
        flops=heads * 12 * rows * keys * HD,
        transcendentals=heads * rows * keys,
        bytes_accessed=2 * feats * (3 * rows + 4 * keys),
    )


def kept_backward(stash, grads, offset, pick):
    _, keys, feats = stash.shape
    rows = grads.shape[1]
    bf16 = jnp.bfloat16
    out_shape = (
        jax.ShapeDtypeStruct((2, rows, feats), bf16),
        jax.ShapeDtypeStruct((2, 2, keys, feats), bf16),
        jax.ShapeDtypeStruct((3, feats), jnp.float32),
    )
    grid_spec = pltpu.PrefetchScalarGridSpec(
        num_scalar_prefetch=1,
        grid=(1,),
        in_specs=[
            pl.BlockSpec((3, keys, feats), lambda i, m: (0, 0, 0)),
            pl.BlockSpec((None, rows, feats), lambda i, m: (m[1], 0, 0)),
        ],
        out_specs=(
            pl.BlockSpec((None, rows, feats), lambda i, m: (0, 0, 0)),
            pl.BlockSpec((None, 2, keys, feats), lambda i, m: (0, 0, 0, 0)),
            pl.BlockSpec((3, feats), lambda i, m: (0, 0)),
        ),
    )
    meta = jnp.stack([offset, pick]).astype(jnp.int32)
    return pl.pallas_call(
        kept_kernel,
        out_shape=out_shape,
        grid_spec=grid_spec,
        cost_estimate=kernel_cost(rows, keys, feats),
        name="kept_backward",
    )(meta, stash, grads)


def held_backward(part, grads, offset, pick, lo):
    rows = grads.shape[1]
    width = part.shape[1]
    assert lo % width == 0
    chunk = lo // width
    keys = (part.shape[0] - rows) // 2
    bf16 = jnp.bfloat16
    grid_spec = pltpu.PrefetchScalarGridSpec(
        num_scalar_prefetch=1,
        grid=(1,),
        in_specs=[
            pl.BlockSpec((part.shape[0], width), lambda i, m: (0, 0)),
            pl.BlockSpec((None, rows, width), lambda i, m: (m[1], 0, chunk)),
        ],
        out_specs=(
            pl.BlockSpec((rows, width), lambda i, m: (0, 0)),
            pl.BlockSpec((2, keys, width), lambda i, m: (0, 0, 0)),
            pl.BlockSpec((3, width), lambda i, m: (0, 0)),
        ),
    )
    meta = jnp.stack([offset, 1 - pick]).astype(jnp.int32)
    return pl.pallas_call(
        held_kernel,
        out_shape=(
            jax.ShapeDtypeStruct((rows, width), bf16),
            jax.ShapeDtypeStruct((2, keys, width), bf16),
            jax.ShapeDtypeStruct((3, width), jnp.float32),
        ),
        grid_spec=grid_spec,
        cost_estimate=kernel_cost(rows, keys, width),
        name="held_backward",
    )(meta, part, grads)


def assemble_kernel(bounds, *refs):
    count = len(bounds)
    q_parts, kv_parts = refs[:count], refs[count:2 * count]
    qg_ref, kv_ref = refs[2 * count + 2:]
    for c, (lo, hi) in enumerate(bounds):
        qg_ref[:, lo:hi] = q_parts[c][...]
        kv_ref[:, :, lo:hi] = kv_parts[c][...]


def assemble(bounds, held_parts, qg, kv):
    rows, feats = qg.shape[1], qg.shape[2]
    keys = kv.shape[2]
    whole = lambda shape: pl.BlockSpec(shape, lambda i: (0,) * len(shape))
    in_specs = (
        [whole(part[0].shape) for part in held_parts]
        + [whole(part[1].shape) for part in held_parts]
        + [pl.BlockSpec(memory_space=pl.ANY), pl.BlockSpec(memory_space=pl.ANY)]
    )
    count = len(held_parts)
    first_alias = 2 * count
    return pl.pallas_call(
        functools.partial(assemble_kernel, tuple(bounds)),
        out_shape=(
            jax.ShapeDtypeStruct(qg.shape, qg.dtype),
            jax.ShapeDtypeStruct(kv.shape, kv.dtype),
        ),
        grid=(1,),
        in_specs=in_specs,
        out_specs=(
            pl.BlockSpec((None, rows, feats), lambda i: (1, 0, 0)),
            pl.BlockSpec((None, 2, keys, feats), lambda i: (1, 0, 0, 0)),
        ),
        input_output_aliases={first_alias: 0, first_alias + 1: 1},
        cost_estimate=pl.CostEstimate(flops=0, transcendentals=0, bytes_accessed=4 * feats * (rows + 2 * keys)),
        name="assemble_held",
    )(*[p[0] for p in held_parts], *[p[1] for p in held_parts], qg, kv)


def chunk_bounds(heads):
    sizes = [heads // 3, heads // 3, heads // 6]
    sizes.append(heads - sum(sizes))
    if min(sizes) < 1:
        sizes = [heads]
    bounds, lo = [], 0
    for size in sizes:
        if lo % size:
            return [(c * HD, (c + 1) * HD) for c in range(heads)] if heads <= 4 else chunk_bounds_even(heads)
        bounds.append((lo * HD, (lo + size) * HD))
        lo += size
    return bounds


def chunk_bounds_even(heads):
    count = next(n for n in (4, 3, 2, 1) if heads % n == 0)
    size = heads // count
    return [(c * size * HD, (c + 1) * size * HD) for c in range(count)]


def chunk_count(heads):
    for count in range(min(MAX_CHUNKS, heads), 0, -1):
        if heads % count == 0:
            return count
    return 1


def body(kept_qkv, held_qkv, sent_grad, order, offsets):
    section_count = lax.axis_size("pipe")
    half_way = section_count // 2
    section_index = lax.axis_index("pipe")
    feats = kept_qkv.shape[-1]
    keys = kept_qkv.shape[-2]
    heads = feats // HD

    owner = (section_index + section_count - half_way) % section_count
    owner_offset = lax.dynamic_index_in_dim(offsets[0], owner, 0, keepdims=False)[1]
    rows = sent_grad.shape[3] * lax.axis_size("tensor")
    held = held_qkv[0, 0]
    held_q = lax.dynamic_slice_in_dim(held[0], owner_offset, rows, 0)
    bounds = chunk_bounds_even(heads)
    fetched = []
    for lo, hi in bounds:
        part = jnp.concatenate([held_q[:, lo:hi], held[1, :, lo:hi], held[2, :, lo:hi]], axis=0)
        fetched.append(from_behind(part, "pipe", half_way))

    arrived = from_behind(sent_grad[0, 0], "pipe", -1)
    tensor_count = lax.axis_size("tensor")
    local_rows = arrived.shape[1]
    split = arrived.reshape(2, local_rows, tensor_count, feats).transpose(2, 0, 1, 3)
    regrouped = lax.all_to_all(split, "tensor", split_axis=0, concat_axis=0, tiled=True)
    regrouped = regrouped.transpose(1, 0, 2, 3).reshape(2, rows, feats)
    pick = order[0, 0]
    section_offsets = lax.dynamic_index_in_dim(offsets[0], section_index, 0, keepdims=False)
    qg, kv, column_sums = kept_backward(kept_qkv[0, 0], regrouped, section_offsets[0], pick)
    first_part, qg, kv, column_sums = lax.optimization_barrier((fetched[0], qg, kv, column_sums))
    fetched = [first_part] + fetched[1:]
    first_part, qg, kv, column_sums = lax.optimization_barrier((fetched[0], qg, kv, column_sums))
    fetched = [first_part] + fetched[1:]
    held_parts = [
        held_backward(part, regrouped, section_offsets[1], pick, lo)
        for (lo, _), part in zip(bounds, fetched)
    ]
    column_sums = column_sums + jnp.concatenate([part[2] for part in held_parts], axis=1)
    qg, kv = assemble(bounds, held_parts, qg, kv)
    query_grad = qg
    key_value_grad = kv
    if lax.axis_size("dp") == 2:
        bias_grad = column_sums + from_behind(column_sums, "dp", 1)
    else:
        bias_grad = lax.psum(column_sums, "dp")
    return (query_grad[None, None], key_value_grad[None, None], bias_grad[None])


def solution(mesh):
    return jax.shard_map(
        body,
        mesh=mesh,
        in_specs=(
            P("dp", "pipe", None, None, "tensor"),
            P("dp", "pipe", None, None, "tensor"),
            P("dp", "pipe", None, "tensor", None),
            P("dp", "pipe"),
            P("dp", None, None),
        ),
        out_specs=(
            P("dp", "pipe", None, None, "tensor"),
            P("dp", "pipe", None, None, None, "tensor"),
            P("pipe", None, "tensor"),
        ),
        check_vma=False,
    )
```

```python
import functools
import math

import jax
import jax.numpy as jnp
from jax import lax
from jax.experimental import pallas as pl
from jax.experimental.pallas import tpu as pltpu
from jax.sharding import PartitionSpec as P

HD = 128
MASK_FILL = -1e30
MAX_CHUNKS = 4
NT_DIMS = (((1,), (1,)), ((), ()))


def from_behind(value, axis, steps):
    count = lax.axis_size(axis)
    pairs = [(source, (source + steps) % count) for source in range(count)]
    return lax.ppermute(value, axis, pairs)


def head_backward(q, k, v, g, visible):
    f32, bf16 = jnp.float32, jnp.bfloat16
    scale = 1.0 / math.sqrt(HD)
    s = lax.dot_general(q, k, NT_DIMS, preferred_element_type=f32) * scale
    s = jnp.where(visible, s, MASK_FILL)
    m = jnp.max(s, axis=1, keepdims=True)
    e = jnp.exp(s - m)
    p = e / jnp.sum(e, axis=1, keepdims=True)
    p_low = p.astype(bf16)
    ctx = jnp.dot(p_low, v, preferred_element_type=f32).astype(bf16)
    delta = jnp.sum(g.astype(f32) * ctx.astype(f32), axis=1, keepdims=True)
    dp = lax.dot_general(g, v, NT_DIMS, preferred_element_type=f32)
    ds = (p * (dp - delta) * scale).astype(bf16)
    dq = jnp.dot(ds, k, preferred_element_type=f32).astype(bf16)
    dk = jnp.dot(ds.T, q, preferred_element_type=f32).astype(bf16)
    dv = jnp.dot(p_low.T, g, preferred_element_type=f32).astype(bf16)
    return dq, dk, dv


def head_loop(offset, load, store):
    rows, keys, heads = load.rows, load.keys, load.heads
    pos = offset + lax.broadcasted_iota(jnp.int32, (rows, keys), 0)
    col = lax.broadcasted_iota(jnp.int32, (rows, keys), 1)
    visible = col <= pos

    def head(h, carry):
        cols = pl.ds(pl.multiple_of(h * HD, HD), HD)
        q, k, v, g = load(cols)
        store(cols, *head_backward(q, k, v, g, visible))
        return carry

    lax.fori_loop(0, heads, head, 0, unroll=True)


class Loader:
    def __init__(self, fn, rows, keys, heads):
        self.fn, self.rows, self.keys, self.heads = fn, rows, keys, heads

    def __call__(self, cols):
        return self.fn(cols)


def store_into(qg_ref, kv_ref, sum_ref, add):
    f32 = jnp.float32

    def store(cols, dq, dk, dv):
        qg_ref[:, cols] = dq
        kv_ref[0, :, cols] = dk
        kv_ref[1, :, cols] = dv
        for row, value in enumerate((dq, dk, dv)):
            total = jnp.sum(value.astype(f32), axis=0, keepdims=True)
            if add:
                total = sum_ref[pl.ds(row, 1), cols] + total
            sum_ref[pl.ds(row, 1), cols] = total

    return store


def kept_kernel(meta_ref, x_ref, g_ref, qg_ref, kv_ref, sum_ref):
    offset = meta_ref[0]
    rows, feats = g_ref.shape
    keys = x_ref.shape[1]
    start = pl.multiple_of(offset, 16)
    load = Loader(
        lambda cols: (x_ref[0, pl.ds(start, rows), cols], x_ref[1, :, cols], x_ref[2, :, cols], g_ref[:, cols]),
        rows, keys, feats // HD,
    )
    head_loop(offset, load, store_into(qg_ref, kv_ref, sum_ref, add=False))


def held_kernel(meta_ref, x_ref, g_ref, qg_ref, kv_ref, sum_ref):
    offset = meta_ref[0]
    rows, feats = g_ref.shape
    keys = (x_ref.shape[0] - rows) // 2
    load = Loader(
        lambda cols: (x_ref[pl.ds(0, rows), cols], x_ref[pl.ds(rows, keys), cols],
                      x_ref[pl.ds(rows + keys, keys), cols], g_ref[:, cols]),
        rows, keys, feats // HD,
    )
    head_loop(offset, load, store_into(qg_ref, kv_ref, sum_ref, add=False))


def kernel_cost(rows, keys, feats):
    heads = feats // HD
    return pl.CostEstimate(
        flops=heads * 12 * rows * keys * HD,
        transcendentals=heads * rows * keys,
        bytes_accessed=2 * feats * (3 * rows + 4 * keys),
    )


def kept_backward(stash, grads, offset, pick):
    _, keys, feats = stash.shape
    rows = grads.shape[1]
    bf16 = jnp.bfloat16
    out_shape = (
        jax.ShapeDtypeStruct((2, rows, feats), bf16),
        jax.ShapeDtypeStruct((2, 2, keys, feats), bf16),
        jax.ShapeDtypeStruct((3, feats), jnp.float32),
    )
    grid_spec = pltpu.PrefetchScalarGridSpec(
        num_scalar_prefetch=1,
        grid=(1,),
        in_specs=[
            pl.BlockSpec((3, keys, feats), lambda i, m: (0, 0, 0)),
            pl.BlockSpec((None, rows, feats), lambda i, m: (m[1], 0, 0)),
        ],
        out_specs=(
            pl.BlockSpec((None, rows, feats), lambda i, m: (0, 0, 0)),
            pl.BlockSpec((None, 2, keys, feats), lambda i, m: (0, 0, 0, 0)),
            pl.BlockSpec((3, feats), lambda i, m: (0, 0)),
        ),
    )
    meta = jnp.stack([offset, pick]).astype(jnp.int32)
    return pl.pallas_call(
        kept_kernel,
        out_shape=out_shape,
        grid_spec=grid_spec,
        cost_estimate=kernel_cost(rows, keys, feats),
        name="kept_backward",
    )(meta, stash, grads)


def held_backward(part, grads, offset, pick, lo):
    rows = grads.shape[1]
    width = part.shape[1]
    assert lo % width == 0
    chunk = lo // width
    keys = (part.shape[0] - rows) // 2
    bf16 = jnp.bfloat16
    first = lo // HD
    grid_spec = pltpu.PrefetchScalarGridSpec(
        num_scalar_prefetch=1,
        grid=(width // HD,),
        in_specs=[
            pl.BlockSpec((part.shape[0], HD), lambda i, m: (0, i)),
            pl.BlockSpec((None, rows, HD), lambda i, m: (m[1], 0, first + i)),
        ],
        out_specs=(
            pl.BlockSpec((rows, HD), lambda i, m: (0, i)),
            pl.BlockSpec((2, keys, HD), lambda i, m: (0, 0, i)),
            pl.BlockSpec((3, HD), lambda i, m: (0, i)),
        ),
    )
    meta = jnp.stack([offset, 1 - pick]).astype(jnp.int32)
    return pl.pallas_call(
        held_kernel,
        out_shape=(
            jax.ShapeDtypeStruct((rows, width), bf16),
            jax.ShapeDtypeStruct((2, keys, width), bf16),
            jax.ShapeDtypeStruct((3, width), jnp.float32),
        ),
        grid_spec=grid_spec,
        cost_estimate=kernel_cost(rows, keys, width),
        name="held_backward",
    )(meta, part, grads)


def assemble_kernel(bounds, *refs):
    count = len(bounds)
    q_parts, kv_parts = refs[:count], refs[count:2 * count]
    qg_ref, kv_ref = refs[2 * count + 2:]
    for c, (lo, hi) in enumerate(bounds):
        qg_ref[:, lo:hi] = q_parts[c][...]
        kv_ref[:, :, lo:hi] = kv_parts[c][...]


def assemble(bounds, held_parts, qg, kv):
    rows, feats = qg.shape[1], qg.shape[2]
    keys = kv.shape[2]
    whole = lambda shape: pl.BlockSpec(shape, lambda i: (0,) * len(shape))
    in_specs = (
        [whole(part[0].shape) for part in held_parts]
        + [whole(part[1].shape) for part in held_parts]
        + [pl.BlockSpec(memory_space=pl.ANY), pl.BlockSpec(memory_space=pl.ANY)]
    )
    count = len(held_parts)
    first_alias = 2 * count
    return pl.pallas_call(
        functools.partial(assemble_kernel, tuple(bounds)),
        out_shape=(
            jax.ShapeDtypeStruct(qg.shape, qg.dtype),
            jax.ShapeDtypeStruct(kv.shape, kv.dtype),
        ),
        grid=(1,),
        in_specs=in_specs,
        out_specs=(
            pl.BlockSpec((None, rows, feats), lambda i: (1, 0, 0)),
            pl.BlockSpec((None, 2, keys, feats), lambda i: (1, 0, 0, 0)),
        ),
        input_output_aliases={first_alias: 0, first_alias + 1: 1},
        cost_estimate=pl.CostEstimate(flops=0, transcendentals=0, bytes_accessed=4 * feats * (rows + 2 * keys)),
        name="assemble_held",
    )(*[p[0] for p in held_parts], *[p[1] for p in held_parts], qg, kv)


def chunk_bounds(heads):
    sizes = [heads // 3, heads // 3, heads // 6]
    sizes.append(heads - sum(sizes))
    if min(sizes) < 1:
        sizes = [heads]
    bounds, lo = [], 0
    for size in sizes:
        if lo % size:
            return [(c * HD, (c + 1) * HD) for c in range(heads)] if heads <= 4 else chunk_bounds_even(heads)
        bounds.append((lo * HD, (lo + size) * HD))
        lo += size
    return bounds


def chunk_bounds_even(heads):
    count = next(n for n in (4, 3, 2, 1) if heads % n == 0)
    size = heads // count
    return [(c * size * HD, (c + 1) * size * HD) for c in range(count)]


def chunk_count(heads):
    for count in range(min(MAX_CHUNKS, heads), 0, -1):
        if heads % count == 0:
            return count
    return 1


def body(kept_qkv, held_qkv, sent_grad, order, offsets):
    section_count = lax.axis_size("pipe")
    half_way = section_count // 2
    section_index = lax.axis_index("pipe")
    feats = kept_qkv.shape[-1]
    keys = kept_qkv.shape[-2]
    heads = feats // HD

    owner = (section_index + section_count - half_way) % section_count
    owner_offset = lax.dynamic_index_in_dim(offsets[0], owner, 0, keepdims=False)[1]
    rows = sent_grad.shape[3] * lax.axis_size("tensor")
    held = held_qkv[0, 0]
    held_q = lax.dynamic_slice_in_dim(held[0], owner_offset, rows, 0)
    bounds = chunk_bounds_even(heads)
    fetched = []
    for lo, hi in bounds:
        part = jnp.concatenate([held_q[:, lo:hi], held[1, :, lo:hi], held[2, :, lo:hi]], axis=0)
        fetched.append(from_behind(part, "pipe", half_way))

    arrived = from_behind(sent_grad[0, 0], "pipe", -1)
    tensor_count = lax.axis_size("tensor")
    local_rows = arrived.shape[1]
    split = arrived.reshape(2, local_rows, tensor_count, feats).transpose(2, 0, 1, 3)
    regrouped = lax.all_to_all(split, "tensor", split_axis=0, concat_axis=0, tiled=True)
    regrouped = regrouped.transpose(1, 0, 2, 3).reshape(2, rows, feats)
    pick = order[0, 0]
    section_offsets = lax.dynamic_index_in_dim(offsets[0], section_index, 0, keepdims=False)
    qg, kv, column_sums = kept_backward(kept_qkv[0, 0], regrouped, section_offsets[0], pick)
    first_part, qg, kv, column_sums = lax.optimization_barrier((fetched[0], qg, kv, column_sums))
    fetched = [first_part] + fetched[1:]
    first_part, qg, kv, column_sums = lax.optimization_barrier((fetched[0], qg, kv, column_sums))
    fetched = [first_part] + fetched[1:]
    held_parts = [
        held_backward(part, regrouped, section_offsets[1], pick, lo)
        for (lo, _), part in zip(bounds, fetched)
    ]
    column_sums = column_sums + jnp.concatenate([part[2] for part in held_parts], axis=1)
    qg, kv = assemble(bounds, held_parts, qg, kv)
    query_grad = qg
    key_value_grad = kv
    if lax.axis_size("dp") == 2:
        bias_grad = column_sums + from_behind(column_sums, "dp", 1)
    else:
        bias_grad = lax.psum(column_sums, "dp")
    return (query_grad[None, None], key_value_grad[None, None], bias_grad[None])


def solution(mesh):
    return jax.shard_map(
        body,
        mesh=mesh,
        in_specs=(
            P("dp", "pipe", None, None, "tensor"),
            P("dp", "pipe", None, None, "tensor"),
            P("dp", "pipe", None, "tensor", None),
            P("dp", "pipe"),
            P("dp", None, None),
        ),
        out_specs=(
            P("dp", "pipe", None, None, "tensor"),
            P("dp", "pipe", None, None, None, "tensor"),
            P("pipe", None, "tensor"),
        ),
        check_vma=False,
    )
```

```python
import functools
import math

import jax
import jax.numpy as jnp
from jax import lax
from jax.experimental import pallas as pl
from jax.experimental.pallas import tpu as pltpu
from jax.sharding import PartitionSpec as P

HD = 128
MASK_FILL = -1e30
MAX_CHUNKS = 4
NT_DIMS = (((1,), (1,)), ((), ()))


def from_behind(value, axis, steps):
    count = lax.axis_size(axis)
    pairs = [(source, (source + steps) % count) for source in range(count)]
    return lax.ppermute(value, axis, pairs)


def head_backward(q, k, v, g, visible):
    f32, bf16 = jnp.float32, jnp.bfloat16
    scale = 1.0 / math.sqrt(HD)
    s = lax.dot_general(q, k, NT_DIMS, preferred_element_type=f32) * scale
    s = jnp.where(visible, s, MASK_FILL)
    m = jnp.max(s, axis=1, keepdims=True)
    e = jnp.exp(s - m)
    p = e / jnp.sum(e, axis=1, keepdims=True)
    p_low = p.astype(bf16)
    ctx = jnp.dot(p_low, v, preferred_element_type=f32).astype(bf16)
    delta = jnp.sum(g.astype(f32) * ctx.astype(f32), axis=1, keepdims=True)
    dp = lax.dot_general(g, v, NT_DIMS, preferred_element_type=f32)
    ds = (p * (dp - delta) * scale).astype(bf16)
    dq = jnp.dot(ds, k, preferred_element_type=f32).astype(bf16)
    dk = jnp.dot(ds.T, q, preferred_element_type=f32).astype(bf16)
    dv = jnp.dot(p_low.T, g, preferred_element_type=f32).astype(bf16)
    return dq, dk, dv


def head_loop(offset, load, store):
    rows, keys, heads = load.rows, load.keys, load.heads
    pos = offset + lax.broadcasted_iota(jnp.int32, (rows, keys), 0)
    col = lax.broadcasted_iota(jnp.int32, (rows, keys), 1)
    visible = col <= pos

    def head(h, carry):
        cols = pl.ds(pl.multiple_of(h * HD, HD), HD)
        q, k, v, g = load(cols)
        store(cols, *head_backward(q, k, v, g, visible))
        return carry

    lax.fori_loop(0, heads, head, 0, unroll=True)


class Loader:
    def __init__(self, fn, rows, keys, heads):
        self.fn, self.rows, self.keys, self.heads = fn, rows, keys, heads

    def __call__(self, cols):
        return self.fn(cols)


def store_into(qg_ref, kv_ref, sum_ref, add):
    f32 = jnp.float32

    def store(cols, dq, dk, dv):
        qg_ref[:, cols] = dq
        kv_ref[0, :, cols] = dk
        kv_ref[1, :, cols] = dv
        for row, value in enumerate((dq, dk, dv)):
            total = jnp.sum(value.astype(f32), axis=0, keepdims=True)
            if add:
                total = sum_ref[pl.ds(row, 1), cols] + total
            sum_ref[pl.ds(row, 1), cols] = total

    return store


def kept_kernel(meta_ref, x_ref, g_ref, qg_ref, kv_ref, sum_ref):
    offset = meta_ref[0]
    rows, feats = g_ref.shape
    keys = x_ref.shape[1]
    start = pl.multiple_of(offset, 16)
    load = Loader(
        lambda cols: (x_ref[0, pl.ds(start, rows), cols], x_ref[1, :, cols], x_ref[2, :, cols], g_ref[:, cols]),
        rows, keys, feats // HD,
    )
    head_loop(offset, load, store_into(qg_ref, kv_ref, sum_ref, add=False))


def held_kernel(meta_ref, x_ref, g_ref, qg_ref, kv_ref, sum_ref):
    offset = meta_ref[0]
    rows, feats = g_ref.shape
    keys = (x_ref.shape[0] - rows) // 2
    load = Loader(
        lambda cols: (x_ref[pl.ds(0, rows), cols], x_ref[pl.ds(rows, keys), cols],
                      x_ref[pl.ds(rows + keys, keys), cols], g_ref[:, cols]),
        rows, keys, feats // HD,
    )
    head_loop(offset, load, store_into(qg_ref, kv_ref, sum_ref, add=False))


def kernel_cost(rows, keys, feats):
    heads = feats // HD
    return pl.CostEstimate(
        flops=heads * 12 * rows * keys * HD,
        transcendentals=heads * rows * keys,
        bytes_accessed=2 * feats * (3 * rows + 4 * keys),
    )


def kept_backward(stash, grads, offset, pick):
    _, keys, feats = stash.shape
    rows = grads.shape[1]
    bf16 = jnp.bfloat16
    out_shape = (
        jax.ShapeDtypeStruct((2, rows, feats), bf16),
        jax.ShapeDtypeStruct((2, 2, keys, feats), bf16),
        jax.ShapeDtypeStruct((3, feats), jnp.float32),
    )
    grid_spec = pltpu.PrefetchScalarGridSpec(
        num_scalar_prefetch=1,
        grid=(1,),
        in_specs=[
            pl.BlockSpec((3, keys, feats), lambda i, m: (0, 0, 0)),
            pl.BlockSpec((None, rows, feats), lambda i, m: (m[1], 0, 0)),
        ],
        out_specs=(
            pl.BlockSpec((None, rows, feats), lambda i, m: (0, 0, 0)),
            pl.BlockSpec((None, 2, keys, feats), lambda i, m: (0, 0, 0, 0)),
            pl.BlockSpec((3, feats), lambda i, m: (0, 0)),
        ),
    )
    meta = jnp.stack([offset, pick]).astype(jnp.int32)
    return pl.pallas_call(
        kept_kernel,
        out_shape=out_shape,
        grid_spec=grid_spec,
        cost_estimate=kernel_cost(rows, keys, feats),
        name="kept_backward",
    )(meta, stash, grads)


def held_backward(part, grads, offset, pick, lo):
    rows = grads.shape[1]
    width = part.shape[1]
    assert lo % width == 0
    chunk = lo // width
    keys = (part.shape[0] - rows) // 2
    bf16 = jnp.bfloat16
    grid_spec = pltpu.PrefetchScalarGridSpec(
        num_scalar_prefetch=1,
        grid=(1,),
        in_specs=[
            pl.BlockSpec((part.shape[0], width), lambda i, m: (0, 0)),
            pl.BlockSpec((None, rows, width), lambda i, m: (m[1], 0, chunk)),
        ],
        out_specs=(
            pl.BlockSpec((rows, width), lambda i, m: (0, 0)),
            pl.BlockSpec((2, keys, width), lambda i, m: (0, 0, 0)),
            pl.BlockSpec((3, width), lambda i, m: (0, 0)),
        ),
    )
    meta = jnp.stack([offset, 1 - pick]).astype(jnp.int32)
    return pl.pallas_call(
        held_kernel,
        out_shape=(
            jax.ShapeDtypeStruct((rows, width), bf16),
            jax.ShapeDtypeStruct((2, keys, width), bf16),
            jax.ShapeDtypeStruct((3, width), jnp.float32),
        ),
        grid_spec=grid_spec,
        cost_estimate=kernel_cost(rows, keys, width),
        name="held_backward",
    )(meta, part, grads)


def assemble_kernel(bounds, *refs):
    count = len(bounds)
    q_parts, kv_parts = refs[:count], refs[count:2 * count]
    qg_ref, kv_ref, sems = refs[2 * count + 2:]
    copies = []
    for c, (lo, hi) in enumerate(bounds):
        cols = pl.ds(lo, hi - lo)
        copies.append(pltpu.make_async_copy(q_parts[c], qg_ref.at[1, :, cols], sems.at[2 * c]))
        copies.append(pltpu.make_async_copy(kv_parts[c], kv_ref.at[1, :, :, cols], sems.at[2 * c + 1]))
    for copy in copies:
        copy.start()
    for copy in copies:
        copy.wait()


def assemble(bounds, held_parts, qg, kv):
    rows, feats = qg.shape[1], qg.shape[2]
    keys = kv.shape[2]
    count = len(held_parts)
    anywhere = pl.BlockSpec(memory_space=pl.ANY)
    return pl.pallas_call(
        functools.partial(assemble_kernel, tuple(bounds)),
        out_shape=(
            jax.ShapeDtypeStruct(qg.shape, qg.dtype),
            jax.ShapeDtypeStruct(kv.shape, kv.dtype),
        ),
        in_specs=[anywhere] * (2 * count + 2),
        out_specs=(anywhere, anywhere),
        scratch_shapes=[pltpu.SemaphoreType.DMA((2 * count,))],
        input_output_aliases={2 * count: 0, 2 * count + 1: 1},
        cost_estimate=pl.CostEstimate(flops=0, transcendentals=0, bytes_accessed=4 * feats * (rows + 2 * keys)),
        name="assemble_held",
    )(*[p[0] for p in held_parts], *[p[1] for p in held_parts], qg, kv)


def chunk_bounds(heads):
    sizes = [heads // 3, heads // 3, heads // 6]
    sizes.append(heads - sum(sizes))
    if min(sizes) < 1:
        sizes = [heads]
    bounds, lo = [], 0
    for size in sizes:
        if lo % size:
            return [(c * HD, (c + 1) * HD) for c in range(heads)] if heads <= 4 else chunk_bounds_even(heads)
        bounds.append((lo * HD, (lo + size) * HD))
        lo += size
    return bounds


def chunk_bounds_even(heads):
    count = next(n for n in (4, 3, 2, 1) if heads % n == 0)
    size = heads // count
    return [(c * size * HD, (c + 1) * size * HD) for c in range(count)]


def chunk_count(heads):
    for count in range(min(MAX_CHUNKS, heads), 0, -1):
        if heads % count == 0:
            return count
    return 1


def body(kept_qkv, held_qkv, sent_grad, order, offsets):
    section_count = lax.axis_size("pipe")
    half_way = section_count // 2
    section_index = lax.axis_index("pipe")
    feats = kept_qkv.shape[-1]
    keys = kept_qkv.shape[-2]
    heads = feats // HD

    owner = (section_index + section_count - half_way) % section_count
    owner_offset = lax.dynamic_index_in_dim(offsets[0], owner, 0, keepdims=False)[1]
    rows = sent_grad.shape[3] * lax.axis_size("tensor")
    held = held_qkv[0, 0]
    held_q = lax.dynamic_slice_in_dim(held[0], owner_offset, rows, 0)
    bounds = chunk_bounds_even(heads)
    fetched = []
    for lo, hi in bounds:
        part = jnp.concatenate([held_q[:, lo:hi], held[1, :, lo:hi], held[2, :, lo:hi]], axis=0)
        fetched.append(from_behind(part, "pipe", half_way))

    arrived = from_behind(sent_grad[0, 0], "pipe", -1)
    tensor_count = lax.axis_size("tensor")
    local_rows = arrived.shape[1]
    split = arrived.reshape(2, local_rows, tensor_count, feats).transpose(2, 0, 1, 3)
    regrouped = lax.all_to_all(split, "tensor", split_axis=0, concat_axis=0, tiled=True)
    regrouped = regrouped.transpose(1, 0, 2, 3).reshape(2, rows, feats)
    pick = order[0, 0]
    section_offsets = lax.dynamic_index_in_dim(offsets[0], section_index, 0, keepdims=False)
    qg, kv, column_sums = kept_backward(kept_qkv[0, 0], regrouped, section_offsets[0], pick)
    first_part, qg, kv, column_sums = lax.optimization_barrier((fetched[0], qg, kv, column_sums))
    fetched = [first_part] + fetched[1:]
    first_part, qg, kv, column_sums = lax.optimization_barrier((fetched[0], qg, kv, column_sums))
    fetched = [first_part] + fetched[1:]
    held_parts = [
        held_backward(part, regrouped, section_offsets[1], pick, lo)
        for (lo, _), part in zip(bounds, fetched)
    ]
    column_sums = column_sums + jnp.concatenate([part[2] for part in held_parts], axis=1)
    qg, kv = assemble(bounds, held_parts, qg, kv)
    query_grad = qg
    key_value_grad = kv
    if lax.axis_size("dp") == 2:
        bias_grad = column_sums + from_behind(column_sums, "dp", 1)
    else:
        bias_grad = lax.psum(column_sums, "dp")
    return (query_grad[None, None], key_value_grad[None, None], bias_grad[None])


def solution(mesh):
    return jax.shard_map(
        body,
        mesh=mesh,
        in_specs=(
            P("dp", "pipe", None, None, "tensor"),
            P("dp", "pipe", None, None, "tensor"),
            P("dp", "pipe", None, "tensor", None),
            P("dp", "pipe"),
            P("dp", None, None),
        ),
        out_specs=(
            P("dp", "pipe", None, None, "tensor"),
            P("dp", "pipe", None, None, None, "tensor"),
            P("pipe", None, "tensor"),
        ),
        check_vma=False,
    )
```

```python
import functools
import math

import jax
import jax.numpy as jnp
from jax import lax
from jax.experimental import pallas as pl
from jax.experimental.pallas import tpu as pltpu
from jax.sharding import PartitionSpec as P

HD = 128
MASK_FILL = -1e30
MAX_CHUNKS = 4
NT_DIMS = (((1,), (1,)), ((), ()))


def from_behind(value, axis, steps):
    count = lax.axis_size(axis)
    pairs = [(source, (source + steps) % count) for source in range(count)]
    return lax.ppermute(value, axis, pairs)


def head_backward(q, k, v, g, visible, visible_t):
    f32, bf16 = jnp.float32, jnp.bfloat16
    scale = 1.0 / math.sqrt(HD)
    s = lax.dot_general(q, k, NT_DIMS, preferred_element_type=f32) * scale
    s = jnp.where(visible, s, MASK_FILL)
    m = jnp.max(s, axis=1, keepdims=True)
    e = jnp.exp(s - m)
    p = e / jnp.sum(e, axis=1, keepdims=True)
    dp = lax.dot_general(g, v, NT_DIMS, preferred_element_type=f32)
    delta = jnp.sum(p.astype(bf16).astype(f32) * dp, axis=1, keepdims=True)
    ds = (p * (dp - delta) * scale).astype(bf16)
    dq = jnp.dot(ds, k, preferred_element_type=f32).astype(bf16)
    st = lax.dot_general(k, q, NT_DIMS, preferred_element_type=f32) * scale
    st = jnp.where(visible_t, st, MASK_FILL)
    mt = jnp.max(st, axis=0, keepdims=True)
    et = jnp.exp(st - mt)
    pt = et / jnp.sum(et, axis=0, keepdims=True)
    pt_low = pt.astype(bf16)
    dpt = lax.dot_general(v, g, NT_DIMS, preferred_element_type=f32)
    delta_t = jnp.sum(pt_low.astype(f32) * dpt, axis=0, keepdims=True)
    dst = (pt * (dpt - delta_t) * scale).astype(bf16)
    dk = jnp.dot(dst, q, preferred_element_type=f32).astype(bf16)
    dv = jnp.dot(pt_low, g, preferred_element_type=f32).astype(bf16)
    return dq, dk, dv


def head_loop(offset, load, store):
    rows, keys, heads = load.rows, load.keys, load.heads
    pos = offset + lax.broadcasted_iota(jnp.int32, (rows, keys), 0)
    col = lax.broadcasted_iota(jnp.int32, (rows, keys), 1)
    visible = col <= pos
    pos_t = offset + lax.broadcasted_iota(jnp.int32, (keys, rows), 1)
    col_t = lax.broadcasted_iota(jnp.int32, (keys, rows), 0)
    visible_t = col_t <= pos_t

    def head(h, carry):
        cols = pl.ds(pl.multiple_of(h * HD, HD), HD)
        q, k, v, g = load(cols)
        store(cols, *head_backward(q, k, v, g, visible, visible_t))
        return carry

    lax.fori_loop(0, heads, head, 0, unroll=True)


class Loader:
    def __init__(self, fn, rows, keys, heads):
        self.fn, self.rows, self.keys, self.heads = fn, rows, keys, heads

    def __call__(self, cols):
        return self.fn(cols)


def store_into(qg_ref, kv_ref, sum_ref, add):
    f32 = jnp.float32

    def store(cols, dq, dk, dv):
        qg_ref[:, cols] = dq
        kv_ref[0, :, cols] = dk
        kv_ref[1, :, cols] = dv
        for row, value in enumerate((dq, dk, dv)):
            total = jnp.sum(value.astype(f32), axis=0, keepdims=True)
            if add:
                total = sum_ref[pl.ds(row, 1), cols] + total
            sum_ref[pl.ds(row, 1), cols] = total

    return store


def kept_kernel(meta_ref, x_ref, g_ref, qg_ref, kv_ref, sum_ref):
    offset = meta_ref[0]
    rows, feats = g_ref.shape
    keys = x_ref.shape[1]
    start = pl.multiple_of(offset, 16)
    load = Loader(
        lambda cols: (x_ref[0, pl.ds(start, rows), cols], x_ref[1, :, cols], x_ref[2, :, cols], g_ref[:, cols]),
        rows, keys, feats // HD,
    )
    head_loop(offset, load, store_into(qg_ref, kv_ref, sum_ref, add=False))


def held_kernel(meta_ref, x_ref, g_ref, qg_ref, kv_ref, sum_ref):
    offset = meta_ref[0]
    rows, feats = g_ref.shape
    keys = (x_ref.shape[0] - rows) // 2
    load = Loader(
        lambda cols: (x_ref[pl.ds(0, rows), cols], x_ref[pl.ds(rows, keys), cols],
                      x_ref[pl.ds(rows + keys, keys), cols], g_ref[:, cols]),
        rows, keys, feats // HD,
    )
    head_loop(offset, load, store_into(qg_ref, kv_ref, sum_ref, add=False))


def kernel_cost(rows, keys, feats):
    heads = feats // HD
    return pl.CostEstimate(
        flops=heads * 12 * rows * keys * HD,
        transcendentals=heads * rows * keys,
        bytes_accessed=2 * feats * (3 * rows + 4 * keys),
    )


def kept_backward(stash, grads, offset, pick):
    _, keys, feats = stash.shape
    rows = grads.shape[1]
    bf16 = jnp.bfloat16
    out_shape = (
        jax.ShapeDtypeStruct((2, rows, feats), bf16),
        jax.ShapeDtypeStruct((2, 2, keys, feats), bf16),
        jax.ShapeDtypeStruct((3, feats), jnp.float32),
    )
    grid_spec = pltpu.PrefetchScalarGridSpec(
        num_scalar_prefetch=1,
        grid=(1,),
        in_specs=[
            pl.BlockSpec((3, keys, feats), lambda i, m: (0, 0, 0)),
            pl.BlockSpec((None, rows, feats), lambda i, m: (m[1], 0, 0)),
        ],
        out_specs=(
            pl.BlockSpec((None, rows, feats), lambda i, m: (0, 0, 0)),
            pl.BlockSpec((None, 2, keys, feats), lambda i, m: (0, 0, 0, 0)),
            pl.BlockSpec((3, feats), lambda i, m: (0, 0)),
        ),
    )
    meta = jnp.stack([offset, pick]).astype(jnp.int32)
    return pl.pallas_call(
        kept_kernel,
        out_shape=out_shape,
        grid_spec=grid_spec,
        cost_estimate=kernel_cost(rows, keys, feats),
        name="kept_backward",
    )(meta, stash, grads)


def held_backward(part, grads, offset, pick, lo):
    rows = grads.shape[1]
    width = part.shape[1]
    assert lo % width == 0
    chunk = lo // width
    keys = (part.shape[0] - rows) // 2
    bf16 = jnp.bfloat16
    grid_spec = pltpu.PrefetchScalarGridSpec(
        num_scalar_prefetch=1,
        grid=(1,),
        in_specs=[
            pl.BlockSpec((part.shape[0], width), lambda i, m: (0, 0)),
            pl.BlockSpec((None, rows, width), lambda i, m: (m[1], 0, chunk)),
        ],
        out_specs=(
            pl.BlockSpec((rows, width), lambda i, m: (0, 0)),
            pl.BlockSpec((2, keys, width), lambda i, m: (0, 0, 0)),
            pl.BlockSpec((3, width), lambda i, m: (0, 0)),
        ),
    )
    meta = jnp.stack([offset, 1 - pick]).astype(jnp.int32)
    return pl.pallas_call(
        held_kernel,
        out_shape=(
            jax.ShapeDtypeStruct((rows, width), bf16),
            jax.ShapeDtypeStruct((2, keys, width), bf16),
            jax.ShapeDtypeStruct((3, width), jnp.float32),
        ),
        grid_spec=grid_spec,
        cost_estimate=kernel_cost(rows, keys, width),
        name="held_backward",
    )(meta, part, grads)


def assemble_kernel(bounds, *refs):
    count = len(bounds)
    q_parts, kv_parts = refs[:count], refs[count:2 * count]
    qg_ref, kv_ref = refs[2 * count + 2:]
    for c, (lo, hi) in enumerate(bounds):
        qg_ref[:, lo:hi] = q_parts[c][...]
        kv_ref[:, :, lo:hi] = kv_parts[c][...]


def assemble(bounds, held_parts, qg, kv):
    rows, feats = qg.shape[1], qg.shape[2]
    keys = kv.shape[2]
    whole = lambda shape: pl.BlockSpec(shape, lambda i: (0,) * len(shape))
    in_specs = (
        [whole(part[0].shape) for part in held_parts]
        + [whole(part[1].shape) for part in held_parts]
        + [pl.BlockSpec(memory_space=pl.ANY), pl.BlockSpec(memory_space=pl.ANY)]
    )
    count = len(held_parts)
    first_alias = 2 * count
    return pl.pallas_call(
        functools.partial(assemble_kernel, tuple(bounds)),
        out_shape=(
            jax.ShapeDtypeStruct(qg.shape, qg.dtype),
            jax.ShapeDtypeStruct(kv.shape, kv.dtype),
        ),
        grid=(1,),
        in_specs=in_specs,
        out_specs=(
            pl.BlockSpec((None, rows, feats), lambda i: (1, 0, 0)),
            pl.BlockSpec((None, 2, keys, feats), lambda i: (1, 0, 0, 0)),
        ),
        input_output_aliases={first_alias: 0, first_alias + 1: 1},
        cost_estimate=pl.CostEstimate(flops=0, transcendentals=0, bytes_accessed=4 * feats * (rows + 2 * keys)),
        name="assemble_held",
    )(*[p[0] for p in held_parts], *[p[1] for p in held_parts], qg, kv)


def chunk_bounds(heads):
    sizes = [heads // 3, heads // 3, heads // 6]
    sizes.append(heads - sum(sizes))
    if min(sizes) < 1:
        sizes = [heads]
    bounds, lo = [], 0
    for size in sizes:
        if lo % size:
            return [(c * HD, (c + 1) * HD) for c in range(heads)] if heads <= 4 else chunk_bounds_even(heads)
        bounds.append((lo * HD, (lo + size) * HD))
        lo += size
    return bounds


def chunk_bounds_even(heads):
    count = next(n for n in (4, 3, 2, 1) if heads % n == 0)
    size = heads // count
    return [(c * size * HD, (c + 1) * size * HD) for c in range(count)]


def chunk_count(heads):
    for count in range(min(MAX_CHUNKS, heads), 0, -1):
        if heads % count == 0:
            return count
    return 1


def body(kept_qkv, held_qkv, sent_grad, order, offsets):
    section_count = lax.axis_size("pipe")
    half_way = section_count // 2
    section_index = lax.axis_index("pipe")
    feats = kept_qkv.shape[-1]
    keys = kept_qkv.shape[-2]
    heads = feats // HD

    owner = (section_index + section_count - half_way) % section_count
    owner_offset = lax.dynamic_index_in_dim(offsets[0], owner, 0, keepdims=False)[1]
    rows = sent_grad.shape[3] * lax.axis_size("tensor")
    held = held_qkv[0, 0]
    held_q = lax.dynamic_slice_in_dim(held[0], owner_offset, rows, 0)
    bounds = chunk_bounds_even(heads)
    fetched = []
    for lo, hi in bounds:
        part = jnp.concatenate([held_q[:, lo:hi], held[1, :, lo:hi], held[2, :, lo:hi]], axis=0)
        fetched.append(from_behind(part, "pipe", half_way))

    arrived = from_behind(sent_grad[0, 0], "pipe", -1)
    tensor_count = lax.axis_size("tensor")
    local_rows = arrived.shape[1]
    split = arrived.reshape(2, local_rows, tensor_count, feats).transpose(2, 0, 1, 3)
    regrouped = lax.all_to_all(split, "tensor", split_axis=0, concat_axis=0, tiled=True)
    regrouped = regrouped.transpose(1, 0, 2, 3).reshape(2, rows, feats)
    pick = order[0, 0]
    section_offsets = lax.dynamic_index_in_dim(offsets[0], section_index, 0, keepdims=False)
    qg, kv, column_sums = kept_backward(kept_qkv[0, 0], regrouped, section_offsets[0], pick)
    first_part, qg, kv, column_sums = lax.optimization_barrier((fetched[0], qg, kv, column_sums))
    fetched = [first_part] + fetched[1:]
    first_part, qg, kv, column_sums = lax.optimization_barrier((fetched[0], qg, kv, column_sums))
    fetched = [first_part] + fetched[1:]
    held_parts = [
        held_backward(part, regrouped, section_offsets[1], pick, lo)
        for (lo, _), part in zip(bounds, fetched)
    ]
    column_sums = column_sums + jnp.concatenate([part[2] for part in held_parts], axis=1)
    qg, kv = assemble(bounds, held_parts, qg, kv)
    query_grad = qg
    key_value_grad = kv
    if lax.axis_size("dp") == 2:
        bias_grad = column_sums + from_behind(column_sums, "dp", 1)
    else:
        bias_grad = lax.psum(column_sums, "dp")
    return (query_grad[None, None], key_value_grad[None, None], bias_grad[None])


def solution(mesh):
    return jax.shard_map(
        body,
        mesh=mesh,
        in_specs=(
            P("dp", "pipe", None, None, "tensor"),
            P("dp", "pipe", None, None, "tensor"),
            P("dp", "pipe", None, "tensor", None),
            P("dp", "pipe"),
            P("dp", None, None),
        ),
        out_specs=(
            P("dp", "pipe", None, None, "tensor"),
            P("dp", "pipe", None, None, None, "tensor"),
            P("pipe", None, "tensor"),
        ),
        check_vma=False,
    )
```

```python
import functools
import math

import jax
import jax.numpy as jnp
from jax import lax
from jax.experimental import pallas as pl
from jax.experimental.pallas import tpu as pltpu
from jax.sharding import PartitionSpec as P

HD = 128
MASK_FILL = -1e30
MAX_CHUNKS = 4
NT_DIMS = (((1,), (1,)), ((), ()))


def from_behind(value, axis, steps):
    count = lax.axis_size(axis)
    pairs = [(source, (source + steps) % count) for source in range(count)]
    return lax.ppermute(value, axis, pairs)


def head_backward(q, k, v, g, visible):
    f32, bf16 = jnp.float32, jnp.bfloat16
    scale = 1.0 / math.sqrt(HD)
    s = lax.dot_general(q, k, NT_DIMS, preferred_element_type=f32) * scale
    s = jnp.where(visible, s, MASK_FILL)
    m = jnp.max(s, axis=1, keepdims=True)
    e = jnp.exp(s - m)
    p = e / jnp.sum(e, axis=1, keepdims=True)
    p_low = p.astype(bf16)
    ctx = jnp.dot(p_low, v, preferred_element_type=f32).astype(bf16)
    delta = jnp.sum(g.astype(f32) * ctx.astype(f32), axis=1, keepdims=True)
    dp = lax.dot_general(g, v, NT_DIMS, preferred_element_type=f32)
    ds = (p * (dp - delta) * scale).astype(bf16)
    dq = jnp.dot(ds, k, preferred_element_type=f32).astype(bf16)
    dk = jnp.dot(ds.T, q, preferred_element_type=f32).astype(bf16)
    dv = jnp.dot(p_low.T, g, preferred_element_type=f32).astype(bf16)
    return dq, dk, dv


def head_loop(offset, load, store):
    rows, keys, heads = load.rows, load.keys, load.heads
    pos = offset + lax.broadcasted_iota(jnp.int32, (rows, keys), 0)
    col = lax.broadcasted_iota(jnp.int32, (rows, keys), 1)
    visible = col <= pos

    def head(h, carry):
        cols = pl.ds(pl.multiple_of(h * HD, HD), HD)
        q, k, v, g = load(cols)
        store(cols, *head_backward(q, k, v, g, visible))
        return carry

    lax.fori_loop(0, heads, head, 0, unroll=True)


class Loader:
    def __init__(self, fn, rows, keys, heads):
        self.fn, self.rows, self.keys, self.heads = fn, rows, keys, heads

    def __call__(self, cols):
        return self.fn(cols)


def store_into(qg_ref, kv_ref, sum_ref, add):
    f32 = jnp.float32

    def store(cols, dq, dk, dv):
        qg_ref[:, cols] = dq
        kv_ref[0, :, cols] = dk
        kv_ref[1, :, cols] = dv
        for row, value in enumerate((dq, dk, dv)):
            total = jnp.sum(value.astype(f32), axis=0, keepdims=True)
            if add:
                total = sum_ref[pl.ds(row, 1), cols] + total
            sum_ref[pl.ds(row, 1), cols] = total

    return store


def kept_kernel(meta_ref, x_ref, g_ref, qg_ref, kv_ref, sum_ref):
    offset = meta_ref[0]
    rows, feats = g_ref.shape
    keys = x_ref.shape[1]
    start = pl.multiple_of(offset, 16)
    load = Loader(
        lambda cols: (x_ref[0, pl.ds(start, rows), cols], x_ref[1, :, cols], x_ref[2, :, cols], g_ref[:, cols]),
        rows, keys, feats // HD,
    )
    head_loop(offset, load, store_into(qg_ref, kv_ref, sum_ref, add=False))


def held_kernel(meta_ref, x_ref, g_ref, qg_ref, kv_ref, sum_ref):
    offset = meta_ref[0]
    rows, feats = g_ref.shape
    keys = (x_ref.shape[0] - rows) // 2
    load = Loader(
        lambda cols: (x_ref[pl.ds(0, rows), cols], x_ref[pl.ds(rows, keys), cols],
                      x_ref[pl.ds(rows + keys, keys), cols], g_ref[:, cols]),
        rows, keys, feats // HD,
    )
    head_loop(offset, load, store_into(qg_ref, kv_ref, sum_ref, add=False))


def kernel_cost(rows, keys, feats):
    heads = feats // HD
    return pl.CostEstimate(
        flops=heads * 12 * rows * keys * HD,
        transcendentals=heads * rows * keys,
        bytes_accessed=2 * feats * (3 * rows + 4 * keys),
    )


def kept_backward(stash, grads, offset, pick):
    _, keys, feats = stash.shape
    rows = grads.shape[1]
    bf16 = jnp.bfloat16
    out_shape = (
        jax.ShapeDtypeStruct((2, rows, feats), bf16),
        jax.ShapeDtypeStruct((2, 2, keys, feats), bf16),
        jax.ShapeDtypeStruct((3, feats), jnp.float32),
    )
    grid_spec = pltpu.PrefetchScalarGridSpec(
        num_scalar_prefetch=1,
        grid=(1,),
        in_specs=[
            pl.BlockSpec((3, keys, feats), lambda i, m: (0, 0, 0)),
            pl.BlockSpec((None, rows, feats), lambda i, m: (m[1], 0, 0)),
        ],
        out_specs=(
            pl.BlockSpec((None, rows, feats), lambda i, m: (0, 0, 0)),
            pl.BlockSpec((None, 2, keys, feats), lambda i, m: (0, 0, 0, 0)),
            pl.BlockSpec((3, feats), lambda i, m: (0, 0)),
        ),
    )
    meta = jnp.stack([offset, pick]).astype(jnp.int32)
    return pl.pallas_call(
        kept_kernel,
        out_shape=out_shape,
        grid_spec=grid_spec,
        cost_estimate=kernel_cost(rows, keys, feats),
        name="kept_backward",
    )(meta, stash, grads)


def held_backward(part, grads, offset, pick, lo):
    rows = grads.shape[1]
    width = part.shape[1]
    assert lo % width == 0
    chunk = lo // width
    keys = (part.shape[0] - rows) // 2
    bf16 = jnp.bfloat16
    grid_spec = pltpu.PrefetchScalarGridSpec(
        num_scalar_prefetch=1,
        grid=(1,),
        in_specs=[
            pl.BlockSpec(memory_space=pltpu.VMEM),
            pl.BlockSpec((None, rows, width), lambda i, m: (m[1], 0, chunk)),
        ],
        out_specs=(
            pl.BlockSpec((rows, width), lambda i, m: (0, 0)),
            pl.BlockSpec((2, keys, width), lambda i, m: (0, 0, 0)),
            pl.BlockSpec((3, width), lambda i, m: (0, 0)),
        ),
    )
    meta = jnp.stack([offset, 1 - pick]).astype(jnp.int32)
    return pl.pallas_call(
        held_kernel,
        out_shape=(
            jax.ShapeDtypeStruct((rows, width), bf16),
            jax.ShapeDtypeStruct((2, keys, width), bf16),
            jax.ShapeDtypeStruct((3, width), jnp.float32),
        ),
        grid_spec=grid_spec,
        cost_estimate=kernel_cost(rows, keys, width),
        name="held_backward",
    )(meta, pltpu.with_memory_space_constraint(part, pltpu.VMEM), grads)


def assemble_kernel(bounds, *refs):
    count = len(bounds)
    q_parts, kv_parts = refs[:count], refs[count:2 * count]
    qg_ref, kv_ref = refs[2 * count + 2:]
    for c, (lo, hi) in enumerate(bounds):
        qg_ref[:, lo:hi] = q_parts[c][...]
        kv_ref[:, :, lo:hi] = kv_parts[c][...]


def assemble(bounds, held_parts, qg, kv):
    rows, feats = qg.shape[1], qg.shape[2]
    keys = kv.shape[2]
    whole = lambda shape: pl.BlockSpec(shape, lambda i: (0,) * len(shape))
    in_specs = (
        [whole(part[0].shape) for part in held_parts]
        + [whole(part[1].shape) for part in held_parts]
        + [pl.BlockSpec(memory_space=pl.ANY), pl.BlockSpec(memory_space=pl.ANY)]
    )
    count = len(held_parts)
    first_alias = 2 * count
    return pl.pallas_call(
        functools.partial(assemble_kernel, tuple(bounds)),
        out_shape=(
            jax.ShapeDtypeStruct(qg.shape, qg.dtype),
            jax.ShapeDtypeStruct(kv.shape, kv.dtype),
        ),
        grid=(1,),
        in_specs=in_specs,
        out_specs=(
            pl.BlockSpec((None, rows, feats), lambda i: (1, 0, 0)),
            pl.BlockSpec((None, 2, keys, feats), lambda i: (1, 0, 0, 0)),
        ),
        input_output_aliases={first_alias: 0, first_alias + 1: 1},
        cost_estimate=pl.CostEstimate(flops=0, transcendentals=0, bytes_accessed=4 * feats * (rows + 2 * keys)),
        name="assemble_held",
    )(*[p[0] for p in held_parts], *[p[1] for p in held_parts], qg, kv)


def chunk_bounds(heads):
    sizes = [heads // 3, heads // 3, heads // 6]
    sizes.append(heads - sum(sizes))
    if min(sizes) < 1:
        sizes = [heads]
    bounds, lo = [], 0
    for size in sizes:
        if lo % size:
            return [(c * HD, (c + 1) * HD) for c in range(heads)] if heads <= 4 else chunk_bounds_even(heads)
        bounds.append((lo * HD, (lo + size) * HD))
        lo += size
    return bounds


def chunk_bounds_even(heads):
    count = next(n for n in (4, 3, 2, 1) if heads % n == 0)
    size = heads // count
    return [(c * size * HD, (c + 1) * size * HD) for c in range(count)]


def chunk_count(heads):
    for count in range(min(MAX_CHUNKS, heads), 0, -1):
        if heads % count == 0:
            return count
    return 1


def body(kept_qkv, held_qkv, sent_grad, order, offsets):
    section_count = lax.axis_size("pipe")
    half_way = section_count // 2
    section_index = lax.axis_index("pipe")
    feats = kept_qkv.shape[-1]
    keys = kept_qkv.shape[-2]
    heads = feats // HD

    owner = (section_index + section_count - half_way) % section_count
    owner_offset = lax.dynamic_index_in_dim(offsets[0], owner, 0, keepdims=False)[1]
    rows = sent_grad.shape[3] * lax.axis_size("tensor")
    held = held_qkv[0, 0]
    held_q = lax.dynamic_slice_in_dim(held[0], owner_offset, rows, 0)
    bounds = chunk_bounds_even(heads)
    fetched = []
    for lo, hi in bounds:
        part = jnp.concatenate([held_q[:, lo:hi], held[1, :, lo:hi], held[2, :, lo:hi]], axis=0)
        fetched.append(from_behind(part, "pipe", half_way))

    arrived = from_behind(sent_grad[0, 0], "pipe", -1)
    tensor_count = lax.axis_size("tensor")
    local_rows = arrived.shape[1]
    split = arrived.reshape(2, local_rows, tensor_count, feats).transpose(2, 0, 1, 3)
    regrouped = lax.all_to_all(split, "tensor", split_axis=0, concat_axis=0, tiled=True)
    regrouped = regrouped.transpose(1, 0, 2, 3).reshape(2, rows, feats)
    pick = order[0, 0]
    section_offsets = lax.dynamic_index_in_dim(offsets[0], section_index, 0, keepdims=False)
    qg, kv, column_sums = kept_backward(kept_qkv[0, 0], regrouped, section_offsets[0], pick)
    first_part, qg, kv, column_sums = lax.optimization_barrier((fetched[0], qg, kv, column_sums))
    fetched = [first_part] + fetched[1:]
    first_part, qg, kv, column_sums = lax.optimization_barrier((fetched[0], qg, kv, column_sums))
    fetched = [first_part] + fetched[1:]
    held_parts = [
        held_backward(part, regrouped, section_offsets[1], pick, lo)
        for (lo, _), part in zip(bounds, fetched)
    ]
    column_sums = column_sums + jnp.concatenate([part[2] for part in held_parts], axis=1)
    qg, kv = assemble(bounds, held_parts, qg, kv)
    query_grad = qg
    key_value_grad = kv
    if lax.axis_size("dp") == 2:
        bias_grad = column_sums + from_behind(column_sums, "dp", 1)
    else:
        bias_grad = lax.psum(column_sums, "dp")
    return (query_grad[None, None], key_value_grad[None, None], bias_grad[None])


def solution(mesh):
    return jax.shard_map(
        body,
        mesh=mesh,
        in_specs=(
            P("dp", "pipe", None, None, "tensor"),
            P("dp", "pipe", None, None, "tensor"),
            P("dp", "pipe", None, "tensor", None),
            P("dp", "pipe"),
            P("dp", None, None),
        ),
        out_specs=(
            P("dp", "pipe", None, None, "tensor"),
            P("dp", "pipe", None, None, None, "tensor"),
            P("pipe", None, "tensor"),
        ),
        check_vma=False,
    )
```

```python
import functools
import math

import jax
import jax.numpy as jnp
from jax import lax
from jax.experimental import pallas as pl
from jax.experimental.pallas import tpu as pltpu
from jax.sharding import PartitionSpec as P

HD = 128
MASK_FILL = -1e30
MAX_CHUNKS = 4
NT_DIMS = (((1,), (1,)), ((), ()))


def from_behind(value, axis, steps):
    count = lax.axis_size(axis)
    pairs = [(source, (source + steps) % count) for source in range(count)]
    return lax.ppermute(value, axis, pairs)


def head_backward(q, k, v, g, visible):
    f32, bf16 = jnp.float32, jnp.bfloat16
    scale = 1.0 / math.sqrt(HD)
    s = lax.dot_general(q, k, NT_DIMS, preferred_element_type=f32) * scale
    s = jnp.where(visible, s, MASK_FILL)
    m = jnp.max(s, axis=1, keepdims=True)
    e = jnp.exp(s - m)
    p = e / jnp.sum(e, axis=1, keepdims=True)
    p_low = p.astype(bf16)
    ctx = jnp.dot(p_low, v, preferred_element_type=f32).astype(bf16)
    delta = jnp.sum(g.astype(f32) * ctx.astype(f32), axis=1, keepdims=True)
    dp = lax.dot_general(g, v, NT_DIMS, preferred_element_type=f32)
    ds = (p * (dp - delta) * scale).astype(bf16)
    dq = jnp.dot(ds, k, preferred_element_type=f32).astype(bf16)
    dk = jnp.dot(ds.T, q, preferred_element_type=f32).astype(bf16)
    dv = jnp.dot(p_low.T, g, preferred_element_type=f32).astype(bf16)
    return dq, dk, dv


def head_loop(offset, load, store):
    rows, keys, heads = load.rows, load.keys, load.heads
    pos = offset + lax.broadcasted_iota(jnp.int32, (rows, keys), 0)
    col = lax.broadcasted_iota(jnp.int32, (rows, keys), 1)
    visible = col <= pos

    def head(h, carry):
        cols = pl.ds(pl.multiple_of(h * HD, HD), HD)
        q, k, v, g = load(cols)
        store(cols, *head_backward(q, k, v, g, visible))
        return carry

    lax.fori_loop(0, heads, head, 0, unroll=True)


class Loader:
    def __init__(self, fn, rows, keys, heads):
        self.fn, self.rows, self.keys, self.heads = fn, rows, keys, heads

    def __call__(self, cols):
        return self.fn(cols)


def store_into(qg_ref, kv_ref, sum_ref, add):
    f32 = jnp.float32

    def store(cols, dq, dk, dv):
        qg_ref[:, cols] = dq
        kv_ref[0, :, cols] = dk
        kv_ref[1, :, cols] = dv
        for row, value in enumerate((dq, dk, dv)):
            total = jnp.sum(value.astype(f32), axis=0, keepdims=True)
            if add:
                total = sum_ref[pl.ds(row, 1), cols] + total
            sum_ref[pl.ds(row, 1), cols] = total

    return store


def kept_kernel(meta_ref, x_ref, g_ref, qg_ref, kv_ref, sum_ref):
    offset = meta_ref[0]
    rows, feats = g_ref.shape
    keys = x_ref.shape[1]
    start = pl.multiple_of(offset, 16)
    load = Loader(
        lambda cols: (x_ref[0, pl.ds(start, rows), cols], x_ref[1, :, cols], x_ref[2, :, cols], g_ref[:, cols]),
        rows, keys, feats // HD,
    )
    head_loop(offset, load, store_into(qg_ref, kv_ref, sum_ref, add=False))


def held_kernel(meta_ref, x_ref, g_ref, qg_ref, kv_ref, sum_ref):
    offset = meta_ref[0]
    rows, feats = g_ref.shape
    keys = (x_ref.shape[0] - rows) // 2
    load = Loader(
        lambda cols: (x_ref[pl.ds(0, rows), cols], x_ref[pl.ds(rows, keys), cols],
                      x_ref[pl.ds(rows + keys, keys), cols], g_ref[:, cols]),
        rows, keys, feats // HD,
    )
    head_loop(offset, load, store_into(qg_ref, kv_ref, sum_ref, add=False))


def kernel_cost(rows, keys, feats):
    heads = feats // HD
    return pl.CostEstimate(
        flops=heads * 12 * rows * keys * HD,
        transcendentals=heads * rows * keys,
        bytes_accessed=2 * feats * (3 * rows + 4 * keys),
    )


def kept_backward(stash, grads, offset, pick):
    _, keys, feats = stash.shape
    rows = grads.shape[1]
    bf16 = jnp.bfloat16
    out_shape = (
        jax.ShapeDtypeStruct((2, rows, feats), bf16),
        jax.ShapeDtypeStruct((2, 2, keys, feats), bf16),
        jax.ShapeDtypeStruct((3, feats), jnp.float32),
    )
    grid_spec = pltpu.PrefetchScalarGridSpec(
        num_scalar_prefetch=1,
        grid=(1,),
        in_specs=[
            pl.BlockSpec((3, keys, feats), lambda i, m: (0, 0, 0)),
            pl.BlockSpec((None, rows, feats), lambda i, m: (m[1], 0, 0)),
        ],
        out_specs=(
            pl.BlockSpec((None, rows, feats), lambda i, m: (0, 0, 0)),
            pl.BlockSpec((None, 2, keys, feats), lambda i, m: (0, 0, 0, 0)),
            pl.BlockSpec((3, feats), lambda i, m: (0, 0)),
        ),
    )
    meta = jnp.stack([offset, pick]).astype(jnp.int32)
    return pl.pallas_call(
        kept_kernel,
        out_shape=out_shape,
        grid_spec=grid_spec,
        cost_estimate=kernel_cost(rows, keys, feats),
        name="kept_backward",
    )(meta, stash, grads)


def held_backward(part, grads, offset, pick, lo):
    rows = grads.shape[1]
    width = part.shape[1]
    assert lo % width == 0
    chunk = lo // width
    keys = (part.shape[0] - rows) // 2
    bf16 = jnp.bfloat16
    grid_spec = pltpu.PrefetchScalarGridSpec(
        num_scalar_prefetch=1,
        grid=(1,),
        in_specs=[
            pl.BlockSpec(memory_space=pltpu.VMEM),
            pl.BlockSpec((None, rows, width), lambda i, m: (m[1], 0, chunk)),
        ],
        out_specs=(
            pl.BlockSpec((rows, width), lambda i, m: (0, 0)),
            pl.BlockSpec((2, keys, width), lambda i, m: (0, 0, 0)),
            pl.BlockSpec((3, width), lambda i, m: (0, 0)),
        ),
    )
    meta = jnp.stack([offset, 1 - pick]).astype(jnp.int32)
    return pl.pallas_call(
        held_kernel,
        out_shape=(
            jax.ShapeDtypeStruct((rows, width), bf16),
            jax.ShapeDtypeStruct((2, keys, width), bf16),
            jax.ShapeDtypeStruct((3, width), jnp.float32),
        ),
        grid_spec=grid_spec,
        cost_estimate=kernel_cost(rows, keys, width),
        name="held_backward",
    )(meta, pltpu.with_memory_space_constraint(part, pltpu.VMEM), grads)


def assemble_kernel(bounds, *refs):
    count = len(bounds)
    q_parts, kv_parts = refs[:count], refs[count:2 * count]
    qg_ref, kv_ref, sems = refs[2 * count + 2:]
    copies = []
    for c, (lo, hi) in enumerate(bounds):
        cols = pl.ds(lo, hi - lo)
        copies.append(pltpu.make_async_copy(q_parts[c], qg_ref.at[pl.ds(0, 1), pl.ds(0, qg_ref.shape[1]), cols], sems.at[2 * c]))
        copies.append(pltpu.make_async_copy(kv_parts[c], kv_ref.at[pl.ds(0, 1), pl.ds(0, 2), pl.ds(0, kv_ref.shape[2]), cols], sems.at[2 * c + 1]))
    for copy in copies:
        copy.start()
    for copy in copies:
        copy.wait()


def assemble(bounds, held_parts, qg, kv):
    rows, feats = qg.shape[1], qg.shape[2]
    keys = kv.shape[2]
    anywhere = pl.BlockSpec(memory_space=pl.ANY)
    count = len(held_parts)
    first_alias = 2 * count
    return pl.pallas_call(
        functools.partial(assemble_kernel, tuple(bounds)),
        out_shape=(
            jax.ShapeDtypeStruct(qg.shape, qg.dtype),
            jax.ShapeDtypeStruct(kv.shape, kv.dtype),
        ),
        grid=(1,),
        in_specs=[anywhere] * (2 * count + 2),
        out_specs=(
            pl.BlockSpec((1, rows, feats), lambda i: (1, 0, 0)),
            pl.BlockSpec((1, 2, keys, feats), lambda i: (1, 0, 0, 0)),
        ),
        scratch_shapes=[pltpu.SemaphoreType.DMA((2 * count,))],
        input_output_aliases={first_alias: 0, first_alias + 1: 1},
        cost_estimate=pl.CostEstimate(flops=0, transcendentals=0, bytes_accessed=4 * feats * (rows + 2 * keys)),
        name="assemble_held",
    )(*[p[0][None] for p in held_parts], *[p[1][None] for p in held_parts], qg, kv)


def chunk_bounds(heads):
    sizes = [heads // 3, heads // 3, heads // 6]
    sizes.append(heads - sum(sizes))
    if min(sizes) < 1:
        sizes = [heads]
    bounds, lo = [], 0
    for size in sizes:
        if lo % size:
            return [(c * HD, (c + 1) * HD) for c in range(heads)] if heads <= 4 else chunk_bounds_even(heads)
        bounds.append((lo * HD, (lo + size) * HD))
        lo += size
    return bounds


def chunk_bounds_even(heads):
    count = next(n for n in (4, 3, 2, 1) if heads % n == 0)
    size = heads // count
    return [(c * size * HD, (c + 1) * size * HD) for c in range(count)]


def chunk_count(heads):
    for count in range(min(MAX_CHUNKS, heads), 0, -1):
        if heads % count == 0:
            return count
    return 1


def body(kept_qkv, held_qkv, sent_grad, order, offsets):
    section_count = lax.axis_size("pipe")
    half_way = section_count // 2
    section_index = lax.axis_index("pipe")
    feats = kept_qkv.shape[-1]
    keys = kept_qkv.shape[-2]
    heads = feats // HD

    owner = (section_index + section_count - half_way) % section_count
    owner_offset = lax.dynamic_index_in_dim(offsets[0], owner, 0, keepdims=False)[1]
    rows = sent_grad.shape[3] * lax.axis_size("tensor")
    held = held_qkv[0, 0]
    held_q = lax.dynamic_slice_in_dim(held[0], owner_offset, rows, 0)
    bounds = chunk_bounds_even(heads)
    fetched = []
    for lo, hi in bounds:
        part = jnp.concatenate([held_q[:, lo:hi], held[1, :, lo:hi], held[2, :, lo:hi]], axis=0)
        fetched.append(from_behind(part, "pipe", half_way))

    arrived = from_behind(sent_grad[0, 0], "pipe", -1)
    tensor_count = lax.axis_size("tensor")
    local_rows = arrived.shape[1]
    split = arrived.reshape(2, local_rows, tensor_count, feats).transpose(2, 0, 1, 3)
    regrouped = lax.all_to_all(split, "tensor", split_axis=0, concat_axis=0, tiled=True)
    regrouped = regrouped.transpose(1, 0, 2, 3).reshape(2, rows, feats)
    pick = order[0, 0]
    section_offsets = lax.dynamic_index_in_dim(offsets[0], section_index, 0, keepdims=False)
    qg, kv, column_sums = kept_backward(kept_qkv[0, 0], regrouped, section_offsets[0], pick)
    first_part, qg, kv, column_sums = lax.optimization_barrier((fetched[0], qg, kv, column_sums))
    fetched = [first_part] + fetched[1:]
    first_part, qg, kv, column_sums = lax.optimization_barrier((fetched[0], qg, kv, column_sums))
    fetched = [first_part] + fetched[1:]
    held_parts = [
        held_backward(part, regrouped, section_offsets[1], pick, lo)
        for (lo, _), part in zip(bounds, fetched)
    ]
    column_sums = column_sums + jnp.concatenate([part[2] for part in held_parts], axis=1)
    qg, kv = assemble(bounds, held_parts, qg, kv)
    query_grad = qg
    key_value_grad = kv
    if lax.axis_size("dp") == 2:
        bias_grad = column_sums + from_behind(column_sums, "dp", 1)
    else:
        bias_grad = lax.psum(column_sums, "dp")
    return (query_grad[None, None], key_value_grad[None, None], bias_grad[None])


def solution(mesh):
    return jax.shard_map(
        body,
        mesh=mesh,
        in_specs=(
            P("dp", "pipe", None, None, "tensor"),
            P("dp", "pipe", None, None, "tensor"),
            P("dp", "pipe", None, "tensor", None),
            P("dp", "pipe"),
            P("dp", None, None),
        ),
        out_specs=(
            P("dp", "pipe", None, None, "tensor"),
            P("dp", "pipe", None, None, None, "tensor"),
            P("pipe", None, "tensor"),
        ),
        check_vma=False,
    )
```
